128 devices in a mesh: lat: 32 (over x, z, core), sub: 4 (over y).
Axes of the slice: x: 4, y: 4, z: 4, core: 2. Of those that a mesh axis runs over, the one named last changes fastest.
Arguments:
- runoff: bfloat16 [262144, 256], P(('lat', 'sub'))
- weight_blocks: bfloat16 [2048, 2, 128, 128], P(('lat', 'sub')), may hold values from -0.1875 to 0.1875
- block_zone: int32 [2048, 2], P(('lat', 'sub')), may hold values from 0 to 511, as said below
- climatology: float32 [65536, 256], P(('lat', 'sub')), may hold values from -6 to 6
- zone_weight: float32 [65536], P(('lat', 'sub')), as said below
Outputs:
- scores: float32 [65536, 256], P(('lat', 'sub'))
- factor: float32 [256, 256], replicated
The draws below stay inside these ranges and needn't reach their ends.
Inputs may be any that keep to these rules, and one draw needn't show every extreme that they name: block_zone[c, k] names a zone block held by the device that holds cell block c, or by the device just before or just after it in the order lat-major, sub-minor; each device's own zone blocks are all named by its own cell blocks. `zone_weight`: positive.
All inputs are finite; a program needn't handle non-finite values.
Results may differ from the reference program's by a relative error of at most 0.0003.
Values sent between devices are 32-bit elements; how exact they have to be, the bound alone decides.
No kernel may reach another device: no remote copies, remote signals or barrier semaphores. Data moves between devices by JAX's collectives and lax.ppermute only.
A program may use at most 64 MiB of HBM per device.

```python
import math
import jax
import jax.numpy as jnp
from jax import lax

BLOCK = 128
DAYS = 256
K = 2
CB_DEV = 16
ZB_DEV = 4
CELL_BLOCKS = 2048
CELLS = 262144
ZONE_BLOCKS = 512
ZONES = 65536


def draw_block_zone(key, part):
    cell_index = jnp.arange(CELL_BLOCKS, dtype=jnp.int32)
    owner = cell_index // CB_DEV
    own_block = owner * ZB_DEV + cell_index % ZB_DEV
    offsets = jax.random.randint(key, (CELL_BLOCKS, K - 1), -ZB_DEV, 2 * ZB_DEV)
    others = jnp.clip(owner[:, None] * ZB_DEV + offsets, 0, ZONE_BLOCKS - 1)
    return jnp.concatenate([own_block[:, None], others], axis=1).astype(jnp.int32)


def draw_runoff(key, part):
    day_scale = jnp.exp(jax.random.uniform(jax.random.fold_in(key, 1), (DAYS,), jnp.float32, math.log(0.5), math.log(5.0)))
    values = jax.random.normal(jax.random.fold_in(key, 2), (CELLS, DAYS), jnp.float32)
    return (values * day_scale[None, :]).astype(jnp.bfloat16)


def draw_zone_weight(key, part):
    ramp = 0.25 + 0.5 * jnp.arange(ZONES, dtype=jnp.float32) / (ZONES - 1)
    rough = jnp.exp(jax.random.uniform(key, (ZONES,), jnp.float32, 0.0, math.log(4.0)))
    return ramp * rough


def shard_levels(key, extent, split, smallest, high):
    gain, own = 1.0, jax.random.fold_in(key, 6)
    for dim, shards_of in split:
        draws = jnp.exp(jax.random.uniform(jax.random.fold_in(own, dim), (shards_of,), jnp.float32, smallest / len(split), high / len(split)))
        gain = gain * jnp.repeat(draws, extent[dim] // shards_of).reshape([-1 if axis == dim else 1 for axis in range(len(extent))])
    return gain


def gaussian(stream_key, shape, spread, limit, shards=(), kind=jnp.bfloat16):
    array = jax.random.normal(stream_key, shape, jnp.float32) * spread
    if len(shards) > 0:
        array = shard_levels(stream_key, shape, shards, -0.22, 0.18) * array
    return jnp.clip(array, min=-limit, max=limit).astype(kind)


def setup_inputs(seed: int = 0) -> dict:
    streams_of = jax.random.split(jax.random.key(seed), 6)
    return {
        "runoff": draw_runoff(jax.random.fold_in(streams_of[5], 71), 0),
        "weight_blocks": gaussian(streams_of[1], (CELL_BLOCKS, K, BLOCK, BLOCK), (2 * CB_DEV * BLOCK // ZB_DEV) ** -0.5, 0.1875, ((0, 128),)),
        "block_zone": draw_block_zone(jax.random.fold_in(streams_of[5], 71), 0),
        "climatology": gaussian(streams_of[3], (ZONES, DAYS), 1.0, 6.0, ((0, 128),), jnp.float32),
        "zone_weight": draw_zone_weight(jax.random.fold_in(streams_of[5], 71), 0),
    }


def reference(runoff, weight_blocks, block_zone, climatology, zone_weight):
    groups = weight_blocks.shape[0] // CB_DEV
    cell_rows = runoff.reshape(groups, CB_DEV, BLOCK, DAYS)
    weights = weight_blocks.reshape(groups, CB_DEV, K, BLOCK, BLOCK)
    targets = block_zone.reshape(groups, CB_DEV * K).astype(jnp.int32)

    def accumulate(table, item):
        rows, blocks_now, where = item
        partial_value = jnp.einsum('ckiz,cit->ckzt', blocks_now.astype(jnp.float32), rows.astype(jnp.float32), precision=lax.Precision.HIGHEST)
        partial_value = partial_value.reshape(CB_DEV * K, BLOCK, DAYS)
        return (table.at[where].add(partial_value), None)
    start_table = jnp.zeros((ZONE_BLOCKS, BLOCK, DAYS), jnp.float32)
    table, unused = lax.scan(accumulate, start_table, (cell_rows, weights, targets))
    aggregated = table.reshape(ZONES, DAYS)
    anomaly = zone_weight[:, None] * (aggregated - climatology)
    gram = jnp.dot(anomaly.T.astype(jnp.float32), anomaly.astype(jnp.float32), precision=lax.Precision.HIGHEST, preferred_element_type=jnp.float32)
    lower = jnp.linalg.cholesky(gram)
    solved = jax.scipy.linalg.solve_triangular(lower, anomaly.T, lower=True)
    root = math.sqrt(ZONES)
    return (solved.T * root, lower.T / root)
```

```python
import itertools
import math

import jax
import jax.numpy as jnp
from jax import lax
from jax.sharding import PartitionSpec as P

exact_mode = lax.Precision.HIGHEST
DEVICE_AXES = ("lat", "sub")


def shifted(value, axis, steps):
    count = lax.axis_size(axis)
    initial, last = (max(0, -steps), min(count, count - steps))
    return lax.ppermute(value, axis, [(source, source + steps) for source in range(initial, last)])


def exchange_stages(count):
    bits = count.bit_length() - 1
    groups, low = [], 0
    for width in (2, 1, 2, 2):
        if low >= bits:
            break
        groups.append(list(range(low, min(bits, low + width))))
        low += width
    if low < bits:
        groups.append(list(range(low, bits)))
    return groups


def all_sum(value, count):
    for group in exchange_stages(count):
        masks = []
        for size in range(1, len(group) + 1):
            for combo in itertools.combinations(group, size):
                masks.append(sum(1 << bit for bit in combo))
        received = [
            lax.ppermute(value, DEVICE_AXES, [(i, i ^ mask) for i in range(count)])
            for mask in masks
        ]
        total = received[0]
        for part in received[1:]:
            total = total + part
        value = value + total
    return value


def pack_gram(gram):
    half = gram.shape[0] // 2
    rows = lax.broadcasted_iota(jnp.int32, (half, half), 0)
    cols = lax.broadcasted_iota(jnp.int32, (half, half), 1)
    g11, g12, g22 = gram[:half, :half], gram[:half, half:], gram[half:, half:]
    tri = jnp.where(rows <= cols, g11, g22)
    diag = jnp.diagonal(g22)
    extra = jnp.zeros((8, 2 * half), gram.dtype).at[0, :half].set(diag)
    return jnp.concatenate([jnp.concatenate([g12, tri], axis=1), extra], axis=0)


def unpack_gram(packed, size):
    half = size // 2
    rows = lax.broadcasted_iota(jnp.int32, (half, half), 0)
    cols = lax.broadcasted_iota(jnp.int32, (half, half), 1)
    g12 = packed[:half, :half]
    tri = packed[:half, half:]
    diag = packed[half, :half]
    g11 = jnp.where(rows <= cols, tri, tri.T)
    g22 = jnp.where(rows > cols, tri, jnp.where(rows < cols, tri.T, jnp.diag(diag)))
    top = jnp.concatenate([g11, g12], axis=1)
    bottom = jnp.concatenate([g12.T, g22], axis=1)
    return jnp.concatenate([top, bottom], axis=0)


def body(runoff, weight_blocks, block_zone, climatology, zone_weight):
    block_count = weight_blocks.shape[0]
    slot_count = weight_blocks.shape[1]
    block_size = weight_blocks.shape[2]
    day_count = runoff.shape[1]
    owned_blocks = climatology.shape[0] // block_size
    device_count = lax.axis_size(DEVICE_AXES)
    device_index = lax.axis_index(DEVICE_AXES)
    cell_rows = runoff.reshape(block_count, block_size, day_count)
    partial_value = jnp.einsum(
        "ckiz,cit->ckzt", weight_blocks, cell_rows, preferred_element_type=jnp.float32
    )
    partial_value = partial_value.reshape(block_count * slot_count, block_size * day_count)
    target_slot = block_zone.reshape(-1) - (device_index - 1) * owned_blocks
    window_slots = jnp.arange(3 * owned_blocks, dtype=jnp.int32)
    one_hot = (window_slots[:, None] == target_slot[None, :]).astype(jnp.float32)
    tables = jnp.dot(
        one_hot, partial_value, precision=exact_mode, preferred_element_type=jnp.float32
    )
    tables = tables.reshape(3 * owned_blocks, block_size, day_count)
    from_before = shifted(tables[2 * owned_blocks :], DEVICE_AXES, 1)
    from_after = shifted(tables[:owned_blocks], DEVICE_AXES, -1)
    summed = tables[owned_blocks : 2 * owned_blocks] + from_before + from_after
    aggregated = summed.reshape(owned_blocks * block_size, day_count)
    anomaly = zone_weight[:, None] * (aggregated - climatology)
    local_gram = jnp.dot(
        anomaly.T, anomaly, precision=exact_mode, preferred_element_type=jnp.float32
    )
    local_gram = 0.5 * (local_gram + local_gram.T)
    total_gram = unpack_gram(all_sum(pack_gram(local_gram), device_count), day_count)
    upper = jnp.linalg.cholesky(total_gram).T
    solved = jax.scipy.linalg.solve_triangular(upper.T, anomaly.T, lower=True)
    root = math.sqrt(anomaly.shape[0] * device_count)
    return (solved.T * root, upper / root)


def solution(mesh):
    return jax.shard_map(
        body,
        mesh=mesh,
        in_specs=(
            P(DEVICE_AXES, None),
            P(DEVICE_AXES, None, None, None),
            P(DEVICE_AXES, None),
            P(DEVICE_AXES, None),
            P(DEVICE_AXES),
        ),
        out_specs=(P(DEVICE_AXES, None), P()),
        check_vma=False,
    )
```

```python
import itertools
import math

import jax
import jax.numpy as jnp
from jax import lax
from jax.sharding import PartitionSpec as P

exact_mode = lax.Precision.HIGHEST
DEVICE_AXES = ("lat", "sub")


def shifted(value, axis, steps):
    count = lax.axis_size(axis)
    initial, last = (max(0, -steps), min(count, count - steps))
    return lax.ppermute(value, axis, [(source, source + steps) for source in range(initial, last)])


def exchange_stages(count):
    bits = count.bit_length() - 1
    groups, low = [], 0
    for width in (2, 1, 2, 2):
        if low >= bits:
            break
        groups.append(list(range(low, min(bits, low + width))))
        low += width
    if low < bits:
        groups.append(list(range(low, bits)))
    return groups


def all_sum(value, count):
    for group in exchange_stages(count):
        masks = []
        for size in range(1, len(group) + 1):
            for combo in itertools.combinations(group, size):
                masks.append(sum(1 << bit for bit in combo))
        received = [
            lax.ppermute(value, DEVICE_AXES, [(i, i ^ mask) for i in range(count)])
            for mask in masks
        ]
        total = received[0]
        for part in received[1:]:
            total = total + part
        value = value + total
    return value


def pack_gram(gram):
    half = gram.shape[0] // 2
    rows = lax.broadcasted_iota(jnp.int32, (half, half), 0)
    cols = lax.broadcasted_iota(jnp.int32, (half, half), 1)
    g11, g12, g22 = gram[:half, :half], gram[:half, half:], gram[half:, half:]
    tri = jnp.where(rows <= cols, g11, g22)
    diag = jnp.diagonal(g22)
    extra = jnp.zeros((8, 2 * half), gram.dtype).at[0, :half].set(diag)
    return jnp.concatenate([jnp.concatenate([g12, tri], axis=1), extra], axis=0)


def unpack_gram(packed, size):
    half = size // 2
    rows = lax.broadcasted_iota(jnp.int32, (half, half), 0)
    cols = lax.broadcasted_iota(jnp.int32, (half, half), 1)
    g12 = packed[:half, :half]
    tri = packed[:half, half:]
    diag = packed[half, :half]
    g11 = jnp.where(rows <= cols, tri, tri.T)
    g22 = jnp.where(rows > cols, tri, jnp.where(rows < cols, tri.T, jnp.diag(diag)))
    top = jnp.concatenate([g11, g12], axis=1)
    bottom = jnp.concatenate([g12.T, g22], axis=1)
    return jnp.concatenate([top, bottom], axis=0)


def blocked_cholesky(gram):
    half = gram.shape[0] // 2
    eye = jnp.eye(half, dtype=gram.dtype)
    zeros = jnp.zeros((half, half), gram.dtype)
    l11 = jnp.linalg.cholesky(gram[:half, :half], symmetrize_input=False)
    l11_inv = lax.linalg.triangular_solve(l11, eye, left_side=True, lower=True)
    l21 = jnp.dot(gram[half:, :half], l11_inv.T, precision=exact_mode)
    schur = gram[half:, half:] - jnp.dot(l21, l21.T, precision=exact_mode)
    l22 = jnp.linalg.cholesky(schur, symmetrize_input=False)
    l22_inv = lax.linalg.triangular_solve(l22, eye, left_side=True, lower=True)
    l21_inv = -jnp.dot(l22_inv, jnp.dot(l21, l11_inv, precision=exact_mode), precision=exact_mode)
    lower = jnp.block([[l11, zeros], [l21, l22]])
    lower_inverse = jnp.block([[l11_inv, zeros], [l21_inv, l22_inv]])
    return lower, lower_inverse


def body(runoff, weight_blocks, block_zone, climatology, zone_weight):
    block_count = weight_blocks.shape[0]
    slot_count = weight_blocks.shape[1]
    block_size = weight_blocks.shape[2]
    day_count = runoff.shape[1]
    owned_blocks = climatology.shape[0] // block_size
    device_count = lax.axis_size(DEVICE_AXES)
    device_index = lax.axis_index(DEVICE_AXES)
    cell_rows = runoff.reshape(block_count, block_size, day_count)
    partial_value = jnp.einsum(
        "ckiz,cit->ckzt", weight_blocks, cell_rows, preferred_element_type=jnp.float32
    )
    partial_value = partial_value.reshape(block_count * slot_count, block_size * day_count)
    target_slot = block_zone.reshape(-1) - (device_index - 1) * owned_blocks
    window_slots = jnp.arange(3 * owned_blocks, dtype=jnp.int32)
    one_hot = (window_slots[:, None] == target_slot[None, :]).astype(jnp.float32)
    tables = jnp.dot(
        one_hot, partial_value, precision=exact_mode, preferred_element_type=jnp.float32
    )
    tables = tables.reshape(3 * owned_blocks, block_size, day_count)
    from_before = shifted(tables[2 * owned_blocks :], DEVICE_AXES, 1)
    from_after = shifted(tables[:owned_blocks], DEVICE_AXES, -1)
    summed = tables[owned_blocks : 2 * owned_blocks] + from_before + from_after
    aggregated = summed.reshape(owned_blocks * block_size, day_count)
    anomaly = zone_weight[:, None] * (aggregated - climatology)
    local_gram = jnp.dot(
        anomaly.T, anomaly, precision=exact_mode, preferred_element_type=jnp.float32
    )
    local_gram = 0.5 * (local_gram + local_gram.T)
    total_gram = unpack_gram(all_sum(pack_gram(local_gram), device_count), day_count)
    lower, lower_inverse = blocked_cholesky(total_gram)
    root = math.sqrt(anomaly.shape[0] * device_count)
    scores = jnp.dot(anomaly, lower_inverse.T * root, precision=exact_mode)
    return (scores, lower.T / root)


def solution(mesh):
    return jax.shard_map(
        body,
        mesh=mesh,
        in_specs=(
            P(DEVICE_AXES, None),
            P(DEVICE_AXES, None, None, None),
            P(DEVICE_AXES, None),
            P(DEVICE_AXES, None),
            P(DEVICE_AXES),
        ),
        out_specs=(P(DEVICE_AXES, None), P()),
        check_vma=False,
    )
```

```python
import itertools
import math

import jax
import jax.numpy as jnp
from jax import lax
from jax.experimental import pallas as pl
from jax.experimental.pallas import tpu as pltpu
from jax.sharding import PartitionSpec as P

exact_mode = lax.Precision.HIGHEST
DEVICE_AXES = ("lat", "sub")


def shifted(value, axis, steps):
    count = lax.axis_size(axis)
    initial, last = (max(0, -steps), min(count, count - steps))
    return lax.ppermute(value, axis, [(source, source + steps) for source in range(initial, last)])


def exchange_stages(count):
    bits = count.bit_length() - 1
    groups, low = [], 0
    for width in (2, 1, 2, 2):
        if low >= bits:
            break
        groups.append(list(range(low, min(bits, low + width))))
        low += width
    if low < bits:
        groups.append(list(range(low, bits)))
    return groups


def all_sum(value, count):
    for group in exchange_stages(count):
        masks = []
        for size in range(1, len(group) + 1):
            for combo in itertools.combinations(group, size):
                masks.append(sum(1 << bit for bit in combo))
        received = [
            lax.ppermute(value, DEVICE_AXES, [(i, i ^ mask) for i in range(count)])
            for mask in masks
        ]
        total = received[0]
        for part in received[1:]:
            total = total + part
        value = value + total
    return value


def pack_gram(gram):
    half = gram.shape[0] // 2
    rows = lax.broadcasted_iota(jnp.int32, (half, half), 0)
    cols = lax.broadcasted_iota(jnp.int32, (half, half), 1)
    g11, g12, g22 = gram[:half, :half], gram[:half, half:], gram[half:, half:]
    tri = jnp.where(rows <= cols, g11, g22)
    diag = jnp.diagonal(g22)
    extra = jnp.zeros((8, 2 * half), gram.dtype).at[0, :half].set(diag)
    return jnp.concatenate([jnp.concatenate([g12, tri], axis=1), extra], axis=0)


def unpack_gram(packed, size):
    half = size // 2
    rows = lax.broadcasted_iota(jnp.int32, (half, half), 0)
    cols = lax.broadcasted_iota(jnp.int32, (half, half), 1)
    g12 = packed[:half, :half]
    tri = packed[:half, half:]
    diag = packed[half, :half]
    g11 = jnp.where(rows <= cols, tri, tri.T)
    g22 = jnp.where(rows > cols, tri, jnp.where(rows < cols, tri.T, jnp.diag(diag)))
    top = jnp.concatenate([g11, g12], axis=1)
    bottom = jnp.concatenate([g12.T, g22], axis=1)
    return jnp.concatenate([top, bottom], axis=0)


def blocked_cholesky(gram):
    half = gram.shape[0] // 2
    eye = jnp.eye(half, dtype=gram.dtype)
    zeros = jnp.zeros((half, half), gram.dtype)
    l11 = jnp.linalg.cholesky(gram[:half, :half], symmetrize_input=False)
    l11_inv = lax.linalg.triangular_solve(l11, eye, left_side=True, lower=True)
    l21 = jnp.dot(gram[half:, :half], l11_inv.T, precision=exact_mode)
    schur = gram[half:, half:] - jnp.dot(l21, l21.T, precision=exact_mode)
    l22 = jnp.linalg.cholesky(schur, symmetrize_input=False)
    l22_inv = lax.linalg.triangular_solve(l22, eye, left_side=True, lower=True)
    l21_inv = -jnp.dot(l22_inv, jnp.dot(l21, l11_inv, precision=exact_mode), precision=exact_mode)
    lower = jnp.block([[l11, zeros], [l21, l22]])
    lower_inverse = jnp.block([[l11_inv, zeros], [l21_inv, l22_inv]])
    return lower, lower_inverse


def aggregate_kernel(slot_ref, weight_ref, rows_ref, out_ref):
    out_ref[...] = jnp.zeros(out_ref.shape, out_ref.dtype)
    block_count, slot_count = weight_ref.shape[0], weight_ref.shape[1]
    for block in range(block_count):
        rows = rows_ref[block]
        for slot in range(slot_count):
            part = lax.dot_general(
                weight_ref[block, slot],
                rows,
                (((0,), (0,)), ((), ())),
                preferred_element_type=jnp.float32,
            )
            target = slot_ref[block * slot_count + slot]
            out_ref[target] = out_ref[target] + part


def aggregate(slots, weight_blocks, cell_rows, window_count):
    block_size = weight_blocks.shape[3]
    day_count = cell_rows.shape[2]
    return pl.pallas_call(
        aggregate_kernel,
        out_shape=jax.ShapeDtypeStruct((window_count, block_size, day_count), jnp.float32),
        in_specs=[
            pl.BlockSpec(memory_space=pltpu.SMEM),
            pl.BlockSpec(memory_space=pltpu.VMEM),
            pl.BlockSpec(memory_space=pltpu.VMEM),
        ],
        out_specs=pl.BlockSpec(memory_space=pltpu.VMEM),
    )(slots, weight_blocks, cell_rows)


def body(runoff, weight_blocks, block_zone, climatology, zone_weight):
    block_count = weight_blocks.shape[0]
    block_size = weight_blocks.shape[2]
    day_count = runoff.shape[1]
    owned_blocks = climatology.shape[0] // block_size
    device_count = lax.axis_size(DEVICE_AXES)
    device_index = lax.axis_index(DEVICE_AXES)
    cell_rows = runoff.reshape(block_count, block_size, day_count)
    target_slot = block_zone.reshape(-1) - (device_index - 1) * owned_blocks
    target_slot = jnp.clip(target_slot, 0, 3 * owned_blocks - 1).astype(jnp.int32)
    tables = aggregate(target_slot, weight_blocks, cell_rows, 3 * owned_blocks)
    from_before = shifted(tables[2 * owned_blocks :], DEVICE_AXES, 1)
    from_after = shifted(tables[:owned_blocks], DEVICE_AXES, -1)
    summed = tables[owned_blocks : 2 * owned_blocks] + from_before + from_after
    aggregated = summed.reshape(owned_blocks * block_size, day_count)
    anomaly = zone_weight[:, None] * (aggregated - climatology)
    local_gram = jnp.dot(
        anomaly.T, anomaly, precision=exact_mode, preferred_element_type=jnp.float32
    )
    local_gram = 0.5 * (local_gram + local_gram.T)
    total_gram = unpack_gram(all_sum(pack_gram(local_gram), device_count), day_count)
    lower, lower_inverse = blocked_cholesky(total_gram)
    root = math.sqrt(anomaly.shape[0] * device_count)
    scores = jnp.dot(anomaly, lower_inverse.T * root, precision=exact_mode)
    return (scores, lower.T / root)


def solution(mesh):
    return jax.shard_map(
        body,
        mesh=mesh,
        in_specs=(
            P(DEVICE_AXES, None),
            P(DEVICE_AXES, None, None, None),
            P(DEVICE_AXES, None),
            P(DEVICE_AXES, None),
            P(DEVICE_AXES),
        ),
        out_specs=(P(DEVICE_AXES, None), P()),
        check_vma=False,
    )
```

```python
import itertools
import math

import jax
import jax.numpy as jnp
from jax import lax
from jax.experimental import pallas as pl
from jax.experimental.pallas import tpu as pltpu
from jax.sharding import PartitionSpec as P

exact_mode = lax.Precision.HIGHEST
DEVICE_AXES = ("lat", "sub")
CORE_BIT = 2


def shifted(value, axis, steps):
    count = lax.axis_size(axis)
    initial, last = (max(0, -steps), min(count, count - steps))
    return lax.ppermute(value, axis, [(source, source + steps) for source in range(initial, last)])


def exchange_stages(count):
    bits = count.bit_length() - 1
    groups, low = [], 0
    for width in (2, 1, 2, 2):
        if low >= bits:
            break
        if low != CORE_BIT:
            groups.append(list(range(low, min(bits, low + width))))
        low += width
    if low < bits:
        groups.append(list(range(low, bits)))
    return groups


def exchange(value, count, mask):
    return lax.ppermute(value, DEVICE_AXES, [(i, i ^ mask) for i in range(count)])


def all_sum(value, count):
    device_index = lax.axis_index(DEVICE_AXES)
    split = count > (1 << CORE_BIT)
    if split:
        core = (device_index >> CORE_BIT) & 1
        half = value.shape[0] // 2
        low, high = value[:half], value[half:]
        kept = jnp.where(core == 0, low, high)
        sent = jnp.where(core == 0, high, low)
        value = kept + exchange(sent, count, 1 << CORE_BIT)
    for group in exchange_stages(count):
        masks = []
        for size in range(1, len(group) + 1):
            for combo in itertools.combinations(group, size):
                masks.append(sum(1 << bit for bit in combo))
        received = [exchange(value, count, mask) for mask in masks]
        total = received[0]
        for part in received[1:]:
            total = total + part
        value = value + total
    if split:
        other = exchange(value, count, 1 << CORE_BIT)
        value = jnp.where(
            core == 0,
            jnp.concatenate([value, other], axis=0),
            jnp.concatenate([other, value], axis=0),
        )
    return value


def pack_gram(gram):
    half = gram.shape[0] // 2
    rows = lax.broadcasted_iota(jnp.int32, (half, half), 0)
    cols = lax.broadcasted_iota(jnp.int32, (half, half), 1)
    g11, g12, g22 = gram[:half, :half], gram[:half, half:], gram[half:, half:]
    tri = jnp.where(rows <= cols, g11, g22)
    diag = jnp.sum(jnp.where(rows == cols, g22, 0.0), axis=0, keepdims=True)
    extra = jnp.zeros((15, 2 * half), gram.dtype)
    extra_row = jnp.concatenate([diag, jnp.zeros_like(diag)], axis=1)
    return jnp.concatenate([jnp.concatenate([g12, tri], axis=1), extra_row, extra], axis=0)


def unpack_gram(packed, size):
    half = size // 2
    rows = lax.broadcasted_iota(jnp.int32, (half, half), 0)
    cols = lax.broadcasted_iota(jnp.int32, (half, half), 1)
    g12 = packed[:half, :half]
    tri = packed[:half, half:]
    diag = packed[half, :half]
    g11 = jnp.where(rows <= cols, tri, tri.T)
    g22 = jnp.where(rows > cols, tri, jnp.where(rows < cols, tri.T, jnp.diag(diag)))
    top = jnp.concatenate([g11, g12], axis=1)
    bottom = jnp.concatenate([g12.T, g22], axis=1)
    return jnp.concatenate([top, bottom], axis=0)


def blocked_cholesky(gram):
    half = gram.shape[0] // 2
    eye = jnp.eye(half, dtype=gram.dtype)
    zeros = jnp.zeros((half, half), gram.dtype)
    l11 = jnp.linalg.cholesky(gram[:half, :half], symmetrize_input=False)
    l11_inv = lax.linalg.triangular_solve(l11, eye, left_side=True, lower=True)
    l21 = jnp.dot(gram[half:, :half], l11_inv.T, precision=exact_mode)
    schur = gram[half:, half:] - jnp.dot(l21, l21.T, precision=exact_mode)
    l22 = jnp.linalg.cholesky(schur, symmetrize_input=False)
    l22_inv = lax.linalg.triangular_solve(l22, eye, left_side=True, lower=True)
    l21_inv = -jnp.dot(l22_inv, jnp.dot(l21, l11_inv, precision=exact_mode), precision=exact_mode)
    lower = jnp.block([[l11, zeros], [l21, l22]])
    lower_inverse = jnp.block([[l11_inv, zeros], [l21_inv, l22_inv]])
    return lower, lower_inverse


def aggregate_kernel(slot_ref, weight_ref, rows_ref, out_ref):
    out_ref[...] = jnp.zeros(out_ref.shape, out_ref.dtype)
    block_count, slot_count = weight_ref.shape[0], weight_ref.shape[1]
    for block in range(block_count):
        rows = rows_ref[block]
        for slot in range(slot_count):
            part = lax.dot_general(
                weight_ref[block, slot],
                rows,
                (((0,), (0,)), ((), ())),
                preferred_element_type=jnp.float32,
            )
            target = slot_ref[block * slot_count + slot]
            out_ref[target] = out_ref[target] + part


def aggregate(slots, weight_blocks, cell_rows, window_count):
    block_size = weight_blocks.shape[3]
    day_count = cell_rows.shape[2]
    return pl.pallas_call(
        aggregate_kernel,
        out_shape=jax.ShapeDtypeStruct((window_count, block_size, day_count), jnp.float32),
        in_specs=[
            pl.BlockSpec(memory_space=pltpu.SMEM),
            pl.BlockSpec(memory_space=pltpu.VMEM),
            pl.BlockSpec(memory_space=pltpu.VMEM),
        ],
        out_specs=pl.BlockSpec(memory_space=pltpu.VMEM),
    )(slots, weight_blocks, cell_rows)


def body(runoff, weight_blocks, block_zone, climatology, zone_weight):
    block_count = weight_blocks.shape[0]
    block_size = weight_blocks.shape[2]
    day_count = runoff.shape[1]
    owned_blocks = climatology.shape[0] // block_size
    device_count = lax.axis_size(DEVICE_AXES)
    device_index = lax.axis_index(DEVICE_AXES)
    cell_rows = runoff.reshape(block_count, block_size, day_count)
    target_slot = block_zone.reshape(-1) - (device_index - 1) * owned_blocks
    target_slot = jnp.clip(target_slot, 0, 3 * owned_blocks - 1).astype(jnp.int32)
    tables = aggregate(target_slot, weight_blocks, cell_rows, 3 * owned_blocks)
    from_before = shifted(tables[2 * owned_blocks :], DEVICE_AXES, 1)
    from_after = shifted(tables[:owned_blocks], DEVICE_AXES, -1)
    summed = tables[owned_blocks : 2 * owned_blocks] + from_before + from_after
    aggregated = summed.reshape(owned_blocks * block_size, day_count)
    anomaly = zone_weight[:, None] * (aggregated - climatology)
    local_gram = jnp.dot(
        anomaly.T, anomaly, precision=exact_mode, preferred_element_type=jnp.float32
    )
    local_gram = 0.5 * (local_gram + local_gram.T)
    total_gram = unpack_gram(all_sum(pack_gram(local_gram), device_count), day_count)
    lower, lower_inverse = blocked_cholesky(total_gram)
    root = math.sqrt(anomaly.shape[0] * device_count)
    scores = jnp.dot(anomaly, lower_inverse.T * root, precision=exact_mode)
    return (scores, lower.T / root)


def solution(mesh):
    return jax.shard_map(
        body,
        mesh=mesh,
        in_specs=(
            P(DEVICE_AXES, None),
            P(DEVICE_AXES, None, None, None),
            P(DEVICE_AXES, None),
            P(DEVICE_AXES, None),
            P(DEVICE_AXES),
        ),
        out_specs=(P(DEVICE_AXES, None), P()),
        check_vma=False,
    )
```

```python
import itertools
import math

import jax
import jax.numpy as jnp
from jax import lax
from jax.experimental import pallas as pl
from jax.experimental.pallas import tpu as pltpu
from jax.sharding import PartitionSpec as P

exact_mode = lax.Precision.HIGHEST
DEVICE_AXES = ("lat", "sub")
CORE_BIT = 2
PANEL = 8


def shifted(value, axis, steps):
    count = lax.axis_size(axis)
    initial, last = (max(0, -steps), min(count, count - steps))
    return lax.ppermute(value, axis, [(source, source + steps) for source in range(initial, last)])


def exchange_stages(count):
    bits = count.bit_length() - 1
    groups, low = [], 0
    for width in (2, 1, 2, 2):
        if low >= bits:
            break
        if low != CORE_BIT:
            groups.append(list(range(low, min(bits, low + width))))
        low += width
    if low < bits:
        groups.append(list(range(low, bits)))
    return groups


def exchange(value, count, mask):
    return lax.ppermute(value, DEVICE_AXES, [(i, i ^ mask) for i in range(count)])


def all_sum(value, count):
    device_index = lax.axis_index(DEVICE_AXES)
    split = count > (1 << CORE_BIT)
    if split:
        core = (device_index >> CORE_BIT) & 1
        half = value.shape[0] // 2
        low, high = value[:half], value[half:]
        kept = jnp.where(core == 0, low, high)
        sent = jnp.where(core == 0, high, low)
        value = kept + exchange(sent, count, 1 << CORE_BIT)
    for group in exchange_stages(count):
        masks = []
        for size in range(1, len(group) + 1):
            for combo in itertools.combinations(group, size):
                masks.append(sum(1 << bit for bit in combo))
        received = [exchange(value, count, mask) for mask in masks]
        total = received[0]
        for part in received[1:]:
            total = total + part
        value = value + total
    if split:
        other = exchange(value, count, 1 << CORE_BIT)
        value = jnp.where(
            core == 0,
            jnp.concatenate([value, other], axis=0),
            jnp.concatenate([other, value], axis=0),
        )
    return value


def pack_gram(gram):
    half = gram.shape[0] // 2
    rows = lax.broadcasted_iota(jnp.int32, (half, half), 0)
    cols = lax.broadcasted_iota(jnp.int32, (half, half), 1)
    g11, g12, g22 = gram[:half, :half], gram[:half, half:], gram[half:, half:]
    tri = jnp.where(rows <= cols, g11, g22)
    diag = jnp.sum(jnp.where(rows == cols, g22, 0.0), axis=0, keepdims=True)
    extra = jnp.zeros((15, 2 * half), gram.dtype)
    extra_row = jnp.concatenate([diag, jnp.zeros_like(diag)], axis=1)
    return jnp.concatenate([jnp.concatenate([g12, tri], axis=1), extra_row, extra], axis=0)


def unpack_gram(packed, size):
    half = size // 2
    rows = lax.broadcasted_iota(jnp.int32, (half, half), 0)
    cols = lax.broadcasted_iota(jnp.int32, (half, half), 1)
    g12 = packed[:half, :half]
    tri = packed[:half, half:]
    diag = packed[half, :half]
    g11 = jnp.where(rows <= cols, tri, tri.T)
    g22 = jnp.where(rows > cols, tri, jnp.where(rows < cols, tri.T, jnp.diag(diag)))
    top = jnp.concatenate([g11, g12], axis=1)
    bottom = jnp.concatenate([g12.T, g22], axis=1)
    return jnp.concatenate([top, bottom], axis=0)


def cholesky_kernel(gram_ref, upper_ref, inverse_ref, work_ref):
    size = gram_ref.shape[0]
    work_ref[...] = gram_ref[...]
    rows = lax.broadcasted_iota(jnp.int32, (size, size), 0)
    cols = lax.broadcasted_iota(jnp.int32, (size, size), 1)
    inverse_ref[...] = jnp.where(rows == cols, 1.0, 0.0).astype(jnp.float32)
    lane = lax.broadcasted_iota(jnp.int32, (1, size), 1)
    sub = lax.broadcasted_iota(jnp.int32, (PANEL, 1), 0)
    row_ids = lax.broadcasted_iota(jnp.int32, (size, 1), 0)

    def panel(index, carry, row0, col0, col1):
        first = pl.multiple_of(index * PANEL, PANEL)
        slab = work_ref[pl.ds(first, PANEL), :]
        inverse_slab = inverse_ref[pl.ds(first, PANEL), :]
        upper_slab = jnp.zeros((PANEL, size), jnp.float32)
        for step in range(PANEL):
            column = first + step
            picked = jnp.sum(jnp.where(lane == column, slab, 0.0), axis=1, keepdims=True)
            scale = lax.rsqrt(picked[step : step + 1, :])
            upper_row = jnp.where(lane >= column, slab[step : step + 1, :] * scale, 0.0)
            inverse_row = inverse_slab[step : step + 1, :] * scale
            coef = jnp.where(sub > step, picked * scale, 0.0)
            slab = slab - coef * upper_row
            inverse_slab = jnp.where(sub == step, inverse_row, inverse_slab - coef * inverse_row)
            upper_slab = jnp.where(sub == step, upper_row, upper_slab)
        upper_ref[pl.ds(first, PANEL), :] = upper_slab
        inverse_ref[pl.ds(first, PANEL), :] = inverse_slab
        lower_cols = jnp.transpose(upper_slab)[row0:]
        lower_cols = jnp.where(row_ids[row0:] >= first + PANEL, lower_cols, 0.0)
        work_ref[row0:, col0:] = work_ref[row0:, col0:] - jnp.dot(
            lower_cols, upper_slab[:, col0:], precision=exact_mode,
            preferred_element_type=jnp.float32,
        )
        inverse_ref[row0:, :col1] = inverse_ref[row0:, :col1] - jnp.dot(
            lower_cols, inverse_slab[:, :col1], precision=exact_mode,
            preferred_element_type=jnp.float32,
        )
        return carry

    quarter = size // 4
    for part in range(4):
        row0 = quarter * part
        col0 = (size // 2) * (part // 2)
        col1 = (size // 2) * (part // 2 + 1)
        lax.fori_loop(
            row0 // PANEL,
            (row0 + quarter) // PANEL,
            lambda index, carry, row0=row0, col0=col0, col1=col1: panel(
                index, carry, row0, col0, col1
            ),
            0,
        )


def cholesky_with_inverse(gram):
    size = gram.shape[0]
    return pl.pallas_call(
        cholesky_kernel,
        out_shape=(
            jax.ShapeDtypeStruct((size, size), jnp.float32),
            jax.ShapeDtypeStruct((size, size), jnp.float32),
        ),
        scratch_shapes=[pltpu.VMEM((size, size), jnp.float32)],
    )(gram)


def aggregate_kernel(slot_ref, weight_ref, rows_ref, out_ref):
    out_ref[...] = jnp.zeros(out_ref.shape, out_ref.dtype)
    block_count, slot_count = weight_ref.shape[0], weight_ref.shape[1]
    for block in range(block_count):
        rows = rows_ref[block]
        for slot in range(slot_count):
            part = lax.dot_general(
                weight_ref[block, slot],
                rows,
                (((0,), (0,)), ((), ())),
                preferred_element_type=jnp.float32,
            )
            target = slot_ref[block * slot_count + slot]
            out_ref[target] = out_ref[target] + part


def aggregate(slots, weight_blocks, cell_rows, window_count):
    block_size = weight_blocks.shape[3]
    day_count = cell_rows.shape[2]
    return pl.pallas_call(
        aggregate_kernel,
        out_shape=jax.ShapeDtypeStruct((window_count, block_size, day_count), jnp.float32),
        in_specs=[
            pl.BlockSpec(memory_space=pltpu.SMEM),
            pl.BlockSpec(memory_space=pltpu.VMEM),
            pl.BlockSpec(memory_space=pltpu.VMEM),
        ],
        out_specs=pl.BlockSpec(memory_space=pltpu.VMEM),
    )(slots, weight_blocks, cell_rows)


def body(runoff, weight_blocks, block_zone, climatology, zone_weight):
    block_count = weight_blocks.shape[0]
    block_size = weight_blocks.shape[2]
    day_count = runoff.shape[1]
    owned_blocks = climatology.shape[0] // block_size
    device_count = lax.axis_size(DEVICE_AXES)
    device_index = lax.axis_index(DEVICE_AXES)
    cell_rows = runoff.reshape(block_count, block_size, day_count)
    target_slot = block_zone.reshape(-1) - (device_index - 1) * owned_blocks
    target_slot = jnp.clip(target_slot, 0, 3 * owned_blocks - 1).astype(jnp.int32)
    tables = aggregate(target_slot, weight_blocks, cell_rows, 3 * owned_blocks)
    from_before = shifted(tables[2 * owned_blocks :], DEVICE_AXES, 1)
    from_after = shifted(tables[:owned_blocks], DEVICE_AXES, -1)
    summed = tables[owned_blocks : 2 * owned_blocks] + from_before + from_after
    aggregated = summed.reshape(owned_blocks * block_size, day_count)
    anomaly = zone_weight[:, None] * (aggregated - climatology)
    local_gram = jnp.dot(
        anomaly.T, anomaly, precision=exact_mode, preferred_element_type=jnp.float32
    )
    local_gram = 0.5 * (local_gram + local_gram.T)
    total_gram = unpack_gram(all_sum(pack_gram(local_gram), device_count), day_count)
    upper, lower_inverse = cholesky_with_inverse(total_gram)
    root = math.sqrt(anomaly.shape[0] * device_count)
    scores = jnp.dot(anomaly, lower_inverse.T * root, precision=exact_mode)
    return (scores, upper / root)


def solution(mesh):
    return jax.shard_map(
        body,
        mesh=mesh,
        in_specs=(
            P(DEVICE_AXES, None),
            P(DEVICE_AXES, None, None, None),
            P(DEVICE_AXES, None),
            P(DEVICE_AXES, None),
            P(DEVICE_AXES),
        ),
        out_specs=(P(DEVICE_AXES, None), P()),
        check_vma=False,
    )
```

```python
import itertools
import math

import jax
import jax.numpy as jnp
from jax import lax
from jax.experimental import pallas as pl
from jax.experimental.pallas import tpu as pltpu
from jax.sharding import PartitionSpec as P

exact_mode = lax.Precision.HIGHEST
DEVICE_AXES = ("lat", "sub")
CORE_BIT = 2
PANEL = 64


def shifted(value, axis, steps):
    count = lax.axis_size(axis)
    initial, last = (max(0, -steps), min(count, count - steps))
    return lax.ppermute(value, axis, [(source, source + steps) for source in range(initial, last)])


def exchange_stages(count):
    bits = count.bit_length() - 1
    groups, low = [], 0
    for width in (2, 1, 2, 2):
        if low >= bits:
            break
        if low != CORE_BIT:
            groups.append(list(range(low, min(bits, low + width))))
        low += width
    if low < bits:
        groups.append(list(range(low, bits)))
    return groups


def exchange(value, count, mask):
    return lax.ppermute(value, DEVICE_AXES, [(i, i ^ mask) for i in range(count)])


def all_sum(value, count):
    device_index = lax.axis_index(DEVICE_AXES)
    split = count > (1 << CORE_BIT)
    if split:
        core = (device_index >> CORE_BIT) & 1
        half = value.shape[0] // 2
        low, high = value[:half], value[half:]
        kept = jnp.where(core == 0, low, high)
        sent = jnp.where(core == 0, high, low)
        value = kept + exchange(sent, count, 1 << CORE_BIT)
    for group in exchange_stages(count):
        masks = []
        for size in range(1, len(group) + 1):
            for combo in itertools.combinations(group, size):
                masks.append(sum(1 << bit for bit in combo))
        received = [exchange(value, count, mask) for mask in masks]
        total = received[0]
        for part in received[1:]:
            total = total + part
        value = value + total
    if split:
        other = exchange(value, count, 1 << CORE_BIT)
        value = jnp.where(
            core == 0,
            jnp.concatenate([value, other], axis=0),
            jnp.concatenate([other, value], axis=0),
        )
    return value


def pack_gram(gram):
    half = gram.shape[0] // 2
    rows = lax.broadcasted_iota(jnp.int32, (half, half), 0)
    cols = lax.broadcasted_iota(jnp.int32, (half, half), 1)
    g11, g12, g22 = gram[:half, :half], gram[:half, half:], gram[half:, half:]
    tri = jnp.where(rows <= cols, g11, g22)
    diag = jnp.sum(jnp.where(rows == cols, g22, 0.0), axis=0, keepdims=True)
    extra = jnp.zeros((15, 2 * half), gram.dtype)
    extra_row = jnp.concatenate([diag, jnp.zeros_like(diag)], axis=1)
    return jnp.concatenate([jnp.concatenate([g12, tri], axis=1), extra_row, extra], axis=0)


def unpack_gram(packed, size):
    half = size // 2
    rows = lax.broadcasted_iota(jnp.int32, (half, half), 0)
    cols = lax.broadcasted_iota(jnp.int32, (half, half), 1)
    g12 = packed[:half, :half]
    tri = packed[:half, half:]
    diag = packed[half, :half]
    g11 = jnp.where(rows <= cols, tri, tri.T)
    g22 = jnp.where(rows > cols, tri, jnp.where(rows < cols, tri.T, jnp.diag(diag)))
    top = jnp.concatenate([g11, g12], axis=1)
    bottom = jnp.concatenate([g12.T, g22], axis=1)
    return jnp.concatenate([top, bottom], axis=0)


def cholesky_kernel(gram_ref, upper_ref, inverse_ref, work_ref):
    size = gram_ref.shape[0]
    work_ref[...] = gram_ref[...]
    rows = lax.broadcasted_iota(jnp.int32, (size, size), 0)
    cols = lax.broadcasted_iota(jnp.int32, (size, size), 1)
    inverse_ref[...] = jnp.where(rows == cols, 1.0, 0.0).astype(jnp.float32)
    upper_ref[...] = jnp.zeros((size, size), jnp.float32)
    sub = lax.broadcasted_iota(jnp.int32, (PANEL, 1), 0)
    row_ids = lax.broadcasted_iota(jnp.int32, (size, 1), 0)
    def panel(index, carry, row0, col0, col1):
        lane = lax.broadcasted_iota(jnp.int32, (1, size - col0), 1) + col0
        first = pl.multiple_of(index * PANEL, PANEL)
        slab = work_ref[pl.ds(first, PANEL), col0:]
        inverse_slab = inverse_ref[pl.ds(first, PANEL), :col1]
        upper_slab = jnp.zeros((PANEL, size - col0), jnp.float32)
        for step in range(PANEL):
            column = first + step
            picked = jnp.sum(jnp.where(lane == column, slab, 0.0), axis=1, keepdims=True)
            scale = lax.rsqrt(picked[step : step + 1, :])
            upper_row = jnp.where(lane >= column, slab[step : step + 1, :] * scale, 0.0)
            inverse_row = inverse_slab[step : step + 1, :] * scale
            coef = jnp.where(sub > step, picked * scale, 0.0)
            slab = slab - coef * upper_row
            inverse_slab = jnp.where(sub == step, inverse_row, inverse_slab - coef * inverse_row)
            upper_slab = jnp.where(sub == step, upper_row, upper_slab)
        upper_ref[pl.ds(first, PANEL), col0:] = upper_slab
        inverse_ref[pl.ds(first, PANEL), :col1] = inverse_slab
        lower_cols = jnp.transpose(upper_slab)[row0 - col0:]
        lower_cols = jnp.where(row_ids[row0:] >= first + PANEL, lower_cols, 0.0)
        work_ref[row0:, col0:] = work_ref[row0:, col0:] - jnp.dot(
            lower_cols, upper_slab, precision=exact_mode, preferred_element_type=jnp.float32)
        inverse_ref[row0:, :col1] = inverse_ref[row0:, :col1] - jnp.dot(
            lower_cols, inverse_slab, precision=exact_mode, preferred_element_type=jnp.float32)
        return carry
    quarter = size // 4
    for part in range(4):
        row0 = quarter * part
        col0 = (size // 2) * (part // 2)
        col1 = (size // 2) * (part // 2 + 1)
        lax.fori_loop(row0 // PANEL, (row0 + quarter) // PANEL,
            lambda index, carry, row0=row0, col0=col0, col1=col1: panel(index, carry, row0, col0, col1), 0)

def cholesky_with_inverse(gram):
    size = gram.shape[0]
    return pl.pallas_call(
        cholesky_kernel,
        out_shape=(
            jax.ShapeDtypeStruct((size, size), jnp.float32),
            jax.ShapeDtypeStruct((size, size), jnp.float32),
        ),
        scratch_shapes=[pltpu.VMEM((size, size), jnp.float32)],
    )(gram)


def aggregate_kernel(slot_ref, weight_ref, rows_ref, out_ref):
    out_ref[...] = jnp.zeros(out_ref.shape, out_ref.dtype)
    block_count, slot_count = weight_ref.shape[0], weight_ref.shape[1]
    for block in range(block_count):
        rows = rows_ref[block]
        for slot in range(slot_count):
            part = lax.dot_general(
                weight_ref[block, slot],
                rows,
                (((0,), (0,)), ((), ())),
                preferred_element_type=jnp.float32,
            )
            target = slot_ref[block * slot_count + slot]
            out_ref[target] = out_ref[target] + part


def aggregate(slots, weight_blocks, cell_rows, window_count):
    block_size = weight_blocks.shape[3]
    day_count = cell_rows.shape[2]
    return pl.pallas_call(
        aggregate_kernel,
        out_shape=jax.ShapeDtypeStruct((window_count, block_size, day_count), jnp.float32),
        in_specs=[
            pl.BlockSpec(memory_space=pltpu.SMEM),
            pl.BlockSpec(memory_space=pltpu.VMEM),
            pl.BlockSpec(memory_space=pltpu.VMEM),
        ],
        out_specs=pl.BlockSpec(memory_space=pltpu.VMEM),
    )(slots, weight_blocks, cell_rows)


def body(runoff, weight_blocks, block_zone, climatology, zone_weight):
    block_count = weight_blocks.shape[0]
    block_size = weight_blocks.shape[2]
    day_count = runoff.shape[1]
    owned_blocks = climatology.shape[0] // block_size
    device_count = lax.axis_size(DEVICE_AXES)
    device_index = lax.axis_index(DEVICE_AXES)
    cell_rows = runoff.reshape(block_count, block_size, day_count)
    target_slot = block_zone.reshape(-1) - (device_index - 1) * owned_blocks
    target_slot = jnp.clip(target_slot, 0, 3 * owned_blocks - 1).astype(jnp.int32)
    tables = aggregate(target_slot, weight_blocks, cell_rows, 3 * owned_blocks)
    from_before = shifted(tables[2 * owned_blocks :], DEVICE_AXES, 1)
    from_after = shifted(tables[:owned_blocks], DEVICE_AXES, -1)
    summed = tables[owned_blocks : 2 * owned_blocks] + from_before + from_after
    aggregated = summed.reshape(owned_blocks * block_size, day_count)
    anomaly = zone_weight[:, None] * (aggregated - climatology)
    local_gram = jnp.dot(
        anomaly.T, anomaly, precision=exact_mode, preferred_element_type=jnp.float32
    )
    local_gram = 0.5 * (local_gram + local_gram.T)
    total_gram = unpack_gram(all_sum(pack_gram(local_gram), device_count), day_count)
    upper, lower_inverse = cholesky_with_inverse(total_gram)
    root = math.sqrt(anomaly.shape[0] * device_count)
    scores = jnp.dot(anomaly, lower_inverse.T * root, precision=exact_mode)
    return (scores, upper / root)


def solution(mesh):
    return jax.shard_map(
        body,
        mesh=mesh,
        in_specs=(
            P(DEVICE_AXES, None),
            P(DEVICE_AXES, None, None, None),
            P(DEVICE_AXES, None),
            P(DEVICE_AXES, None),
            P(DEVICE_AXES),
        ),
        out_specs=(P(DEVICE_AXES, None), P()),
        check_vma=False,
    )
```

```python
import itertools
import math

import jax
import jax.numpy as jnp
from jax import lax
from jax.experimental import pallas as pl
from jax.experimental.pallas import tpu as pltpu
from jax.sharding import PartitionSpec as P

exact_mode = lax.Precision.HIGHEST
DEVICE_AXES = ("lat", "sub")
CORE_BIT = 2
PANEL = 64


def shifted(value, axis, steps):
    count = lax.axis_size(axis)
    initial, last = (max(0, -steps), min(count, count - steps))
    return lax.ppermute(value, axis, [(source, source + steps) for source in range(initial, last)])


def exchange_stages(count):
    bits = count.bit_length() - 1
    groups, low = [], 0
    for width in (2, 1, 2, 2):
        if low >= bits:
            break
        if low != CORE_BIT:
            groups.append(list(range(low, min(bits, low + width))))
        low += width
    if low < bits:
        groups.append(list(range(low, bits)))
    return groups


def exchange(value, count, mask):
    return lax.ppermute(value, DEVICE_AXES, [(i, i ^ mask) for i in range(count)])


def all_sum(value, count):
    device_index = lax.axis_index(DEVICE_AXES)
    split = count > (1 << CORE_BIT)
    if split:
        core = (device_index >> CORE_BIT) & 1
        half = value.shape[0] // 2
        low, high = value[:half], value[half:]
        kept = jnp.where(core == 0, low, high)
        sent = jnp.where(core == 0, high, low)
        value = kept + exchange(sent, count, 1 << CORE_BIT)
    for group in exchange_stages(count):
        masks = []
        for size in range(1, len(group) + 1):
            for combo in itertools.combinations(group, size):
                masks.append(sum(1 << bit for bit in combo))
        received = [exchange(value, count, mask) for mask in masks]
        total = received[0]
        for part in received[1:]:
            total = total + part
        value = value + total
    if split:
        other = exchange(value, count, 1 << CORE_BIT)
        value = jnp.where(
            core == 0,
            jnp.concatenate([value, other], axis=0),
            jnp.concatenate([other, value], axis=0),
        )
    return value


def pack_gram(gram):
    half = gram.shape[0] // 2
    rows = lax.broadcasted_iota(jnp.int32, (half, half), 0)
    cols = lax.broadcasted_iota(jnp.int32, (half, half), 1)
    g11, g12, g22 = gram[:half, :half], gram[:half, half:], gram[half:, half:]
    tri = jnp.where(rows <= cols, g11, g22)
    diag = jnp.sum(jnp.where(rows == cols, g22, 0.0), axis=0, keepdims=True)
    extra = jnp.zeros((15, 2 * half), gram.dtype)
    extra_row = jnp.concatenate([diag, jnp.zeros_like(diag)], axis=1)
    return jnp.concatenate([jnp.concatenate([g12, tri], axis=1), extra_row, extra], axis=0)


def unpack_gram(packed, size):
    half = size // 2
    rows = lax.broadcasted_iota(jnp.int32, (half, half), 0)
    cols = lax.broadcasted_iota(jnp.int32, (half, half), 1)
    g12 = packed[:half, :half]
    tri = packed[:half, half:]
    diag = packed[half, :half]
    g11 = jnp.where(rows <= cols, tri, tri.T)
    g22 = jnp.where(rows > cols, tri, jnp.where(rows < cols, tri.T, jnp.diag(diag)))
    top = jnp.concatenate([g11, g12], axis=1)
    bottom = jnp.concatenate([g12.T, g22], axis=1)
    return jnp.concatenate([top, bottom], axis=0)


def cholesky_kernel(gram_ref, upper_ref, inverse_ref, work_ref):
    size = gram_ref.shape[0]
    work_ref[...] = gram_ref[...]
    rows = lax.broadcasted_iota(jnp.int32, (size, size), 0)
    cols = lax.broadcasted_iota(jnp.int32, (size, size), 1)
    inverse_ref[...] = jnp.where(rows == cols, 1.0, 0.0).astype(jnp.float32)
    upper_ref[...] = jnp.zeros((size, size), jnp.float32)
    sub = lax.broadcasted_iota(jnp.int32, (PANEL, 1), 0)
    row_ids = lax.broadcasted_iota(jnp.int32, (size, 1), 0)
    def panel(first, row0, col0, col1):
        lane = lax.broadcasted_iota(jnp.int32, (1, size - col0), 1) + col0
        slab = work_ref[first:first + PANEL, col0:]
        inverse_slab = inverse_ref[first:first + PANEL, :col1]
        upper_slab = jnp.zeros((PANEL, size - col0), jnp.float32)
        for step in range(PANEL):
            column = first + step
            picked = slab[:, column - col0:column - col0 + 1]
            scale = lax.rsqrt(picked[step : step + 1, :])
            upper_row = jnp.where(lane >= column, slab[step : step + 1, :] * scale, 0.0)
            inverse_row = inverse_slab[step : step + 1, :] * scale
            coef = jnp.where(sub > step, picked * scale, 0.0)
            slab = slab - coef * upper_row
            inverse_slab = jnp.where(sub == step, inverse_row, inverse_slab - coef * inverse_row)
            upper_slab = jnp.where(sub == step, upper_row, upper_slab)
        upper_ref[first:first + PANEL, col0:] = upper_slab
        inverse_ref[first:first + PANEL, :col1] = inverse_slab
        lower_cols = jnp.transpose(upper_slab)[row0 - col0:]
        lower_cols = jnp.where(row_ids[row0:] >= first + PANEL, lower_cols, 0.0)
        work_ref[row0:, col0:] = work_ref[row0:, col0:] - jnp.dot(
            lower_cols, upper_slab, precision=exact_mode, preferred_element_type=jnp.float32)
        inverse_ref[row0:, :col1] = inverse_ref[row0:, :col1] - jnp.dot(
            lower_cols, inverse_slab, precision=exact_mode, preferred_element_type=jnp.float32)

    quarter = size // 4
    for part in range(4):
        row0 = quarter * part
        col0 = (size // 2) * (part // 2)
        col1 = (size // 2) * (part // 2 + 1)
        for first in range(row0, row0 + quarter, PANEL):
            panel(first, row0, col0, col1)


def cholesky_with_inverse(gram):
    size = gram.shape[0]
    return pl.pallas_call(
        cholesky_kernel,
        out_shape=(
            jax.ShapeDtypeStruct((size, size), jnp.float32),
            jax.ShapeDtypeStruct((size, size), jnp.float32),
        ),
        scratch_shapes=[pltpu.VMEM((size, size), jnp.float32)],
    )(gram)


def aggregate_kernel(slot_ref, weight_ref, rows_ref, out_ref):
    out_ref[...] = jnp.zeros(out_ref.shape, out_ref.dtype)
    block_count, slot_count = weight_ref.shape[0], weight_ref.shape[1]
    for block in range(block_count):
        rows = rows_ref[block]
        for slot in range(slot_count):
            part = lax.dot_general(
                weight_ref[block, slot],
                rows,
                (((0,), (0,)), ((), ())),
                preferred_element_type=jnp.float32,
            )
            target = slot_ref[block * slot_count + slot]
            out_ref[target] = out_ref[target] + part


def aggregate(slots, weight_blocks, cell_rows, window_count):
    block_size = weight_blocks.shape[3]
    day_count = cell_rows.shape[2]
    return pl.pallas_call(
        aggregate_kernel,
        out_shape=jax.ShapeDtypeStruct((window_count, block_size, day_count), jnp.float32),
        in_specs=[
            pl.BlockSpec(memory_space=pltpu.SMEM),
            pl.BlockSpec(memory_space=pltpu.VMEM),
            pl.BlockSpec(memory_space=pltpu.VMEM),
        ],
        out_specs=pl.BlockSpec(memory_space=pltpu.VMEM),
    )(slots, weight_blocks, cell_rows)


def body(runoff, weight_blocks, block_zone, climatology, zone_weight):
    block_count = weight_blocks.shape[0]
    block_size = weight_blocks.shape[2]
    day_count = runoff.shape[1]
    owned_blocks = climatology.shape[0] // block_size
    device_count = lax.axis_size(DEVICE_AXES)
    device_index = lax.axis_index(DEVICE_AXES)
    cell_rows = runoff.reshape(block_count, block_size, day_count)
    target_slot = block_zone.reshape(-1) - (device_index - 1) * owned_blocks
    target_slot = jnp.clip(target_slot, 0, 3 * owned_blocks - 1).astype(jnp.int32)
    tables = aggregate(target_slot, weight_blocks, cell_rows, 3 * owned_blocks)
    from_before = shifted(tables[2 * owned_blocks :], DEVICE_AXES, 1)
    from_after = shifted(tables[:owned_blocks], DEVICE_AXES, -1)
    summed = tables[owned_blocks : 2 * owned_blocks] + from_before + from_after
    aggregated = summed.reshape(owned_blocks * block_size, day_count)
    anomaly = zone_weight[:, None] * (aggregated - climatology)
    local_gram = jnp.dot(
        anomaly.T, anomaly, precision=exact_mode, preferred_element_type=jnp.float32
    )
    local_gram = 0.5 * (local_gram + local_gram.T)
    total_gram = unpack_gram(all_sum(pack_gram(local_gram), device_count), day_count)
    upper, lower_inverse = cholesky_with_inverse(total_gram)
    root = math.sqrt(anomaly.shape[0] * device_count)
    scores = jnp.dot(anomaly, lower_inverse.T * root, precision=exact_mode)
    return (scores, upper / root)


def solution(mesh):
    return jax.shard_map(
        body,
        mesh=mesh,
        in_specs=(
            P(DEVICE_AXES, None),
            P(DEVICE_AXES, None, None, None),
            P(DEVICE_AXES, None),
            P(DEVICE_AXES, None),
            P(DEVICE_AXES),
        ),
        out_specs=(P(DEVICE_AXES, None), P()),
        check_vma=False,
    )
```

```python
import functools
import itertools
import math

import jax
import jax.numpy as jnp
from jax import lax
from jax.experimental import pallas as pl
from jax.experimental.pallas import tpu as pltpu
from jax.sharding import PartitionSpec as P

exact_mode = lax.Precision.HIGHEST
DEVICE_AXES = ("lat", "sub")
CORE_BIT = 2
PANEL = 64


def shifted(value, axis, steps):
    count = lax.axis_size(axis)
    initial, last = (max(0, -steps), min(count, count - steps))
    return lax.ppermute(value, axis, [(source, source + steps) for source in range(initial, last)])


def exchange_stages(count):
    bits = count.bit_length() - 1
    groups, low = [], 0
    for width in (2, 1, 2, 2):
        if low >= bits:
            break
        if low != CORE_BIT:
            groups.append(list(range(low, min(bits, low + width))))
        low += width
    if low < bits:
        groups.append(list(range(low, bits)))
    return groups


def exchange(value, count, mask):
    return lax.ppermute(value, DEVICE_AXES, [(i, i ^ mask) for i in range(count)])


def all_sum(value, count):
    device_index = lax.axis_index(DEVICE_AXES)
    split = count > (1 << CORE_BIT)
    if split:
        core = (device_index >> CORE_BIT) & 1
        half = value.shape[0] // 2
        low, high = value[:half], value[half:]
        kept = jnp.where(core == 0, low, high)
        sent = jnp.where(core == 0, high, low)
        value = kept + exchange(sent, count, 1 << CORE_BIT)
    for group in exchange_stages(count):
        masks = []
        for size in range(1, len(group) + 1):
            for combo in itertools.combinations(group, size):
                masks.append(sum(1 << bit for bit in combo))
        received = [exchange(value, count, mask) for mask in masks]
        total = received[0]
        for part in received[1:]:
            total = total + part
        value = value + total
    if split:
        other = exchange(value, count, 1 << CORE_BIT)
        value = jnp.where(
            core == 0,
            jnp.concatenate([value, other], axis=0),
            jnp.concatenate([other, value], axis=0),
        )
    return value


def pack_gram(gram):
    half = gram.shape[0] // 2
    rows = lax.broadcasted_iota(jnp.int32, (half, half), 0)
    cols = lax.broadcasted_iota(jnp.int32, (half, half), 1)
    g11, g12, g22 = gram[:half, :half], gram[:half, half:], gram[half:, half:]
    tri = jnp.where(rows <= cols, g11, g22)
    diag = jnp.sum(jnp.where(rows == cols, g22, 0.0), axis=0, keepdims=True)
    extra = jnp.zeros((15, 2 * half), gram.dtype)
    extra_row = jnp.concatenate([diag, jnp.zeros_like(diag)], axis=1)
    return jnp.concatenate([jnp.concatenate([g12, tri], axis=1), extra_row, extra], axis=0)


def unpack_gram(packed, size):
    half = size // 2
    rows = lax.broadcasted_iota(jnp.int32, (half, half), 0)
    cols = lax.broadcasted_iota(jnp.int32, (half, half), 1)
    g12 = packed[:half, :half]
    tri = packed[:half, half:]
    diag = packed[half, :half]
    g11 = jnp.where(rows <= cols, tri, tri.T)
    g22 = jnp.where(rows > cols, tri, jnp.where(rows < cols, tri.T, jnp.diag(diag)))
    top = jnp.concatenate([g11, g12], axis=1)
    bottom = jnp.concatenate([g12.T, g22], axis=1)
    return jnp.concatenate([top, bottom], axis=0)


def cholesky_kernel(gram_ref, upper_ref, inverse_ref, work_ref, *, factor_scale, inverse_scale):
    size = gram_ref.shape[0]
    work_ref[...] = gram_ref[...]
    rows = lax.broadcasted_iota(jnp.int32, (size, size), 0)
    cols = lax.broadcasted_iota(jnp.int32, (size, size), 1)
    inverse_ref[...] = jnp.where(rows == cols, 1.0, 0.0).astype(jnp.float32)
    upper_ref[...] = jnp.zeros((size, size), jnp.float32)
    sub = lax.broadcasted_iota(jnp.int32, (PANEL, 1), 0)
    row_ids = lax.broadcasted_iota(jnp.int32, (size, 1), 0)
    def panel(first, row0, col0, col1):
        lane = lax.broadcasted_iota(jnp.int32, (1, size - col0), 1) + col0
        slab = work_ref[first:first + PANEL, col0:]
        inverse_slab = inverse_ref[first:first + PANEL, :col1]
        upper_slab = jnp.zeros((PANEL, size - col0), jnp.float32)
        for step in range(PANEL):
            column = first + step
            picked = slab[:, column - col0:column - col0 + 1]
            scale = lax.rsqrt(picked[step : step + 1, :])
            upper_row = jnp.where(lane >= column, slab[step : step + 1, :] * scale, 0.0)
            inverse_row = inverse_slab[step : step + 1, :] * scale
            coef = jnp.where(sub > step, picked * scale, 0.0)
            slab = slab - coef * upper_row
            inverse_slab = jnp.where(sub == step, inverse_row, inverse_slab - coef * inverse_row)
            upper_slab = jnp.where(sub == step, upper_row, upper_slab)
        upper_ref[first:first + PANEL, col0:] = upper_slab * factor_scale
        inverse_ref[first:first + PANEL, :col1] = inverse_slab * inverse_scale
        lower_cols = jnp.transpose(upper_slab)[row0 - col0:]
        lower_cols = jnp.where(row_ids[row0:] >= first + PANEL, lower_cols, 0.0)
        work_ref[row0:, col0:] = work_ref[row0:, col0:] - jnp.dot(
            lower_cols, upper_slab, precision=exact_mode, preferred_element_type=jnp.float32)
        inverse_ref[row0:, :col1] = inverse_ref[row0:, :col1] - jnp.dot(
            lower_cols, inverse_slab, precision=exact_mode, preferred_element_type=jnp.float32)

    quarter = size // 4
    for part in range(4):
        row0 = quarter * part
        col0 = (size // 2) * (part // 2)
        col1 = (size // 2) * (part // 2 + 1)
        for first in range(row0, row0 + quarter, PANEL):
            panel(first, row0, col0, col1)


def cholesky_with_inverse(gram, root):
    size = gram.shape[0]
    return pl.pallas_call(
        functools.partial(cholesky_kernel, factor_scale=1.0 / root, inverse_scale=root),
        out_shape=(
            jax.ShapeDtypeStruct((size, size), jnp.float32),
            jax.ShapeDtypeStruct((size, size), jnp.float32),
        ),
        scratch_shapes=[pltpu.VMEM((size, size), jnp.float32)],
    )(gram)


def aggregate_kernel(zone_ref, base_ref, weight_ref, rows_ref, before_ref, own_ref, after_ref):
    owned = own_ref.shape[0]
    tables = (before_ref, own_ref, after_ref)
    for table in tables:
        table[...] = jnp.zeros(table.shape, table.dtype)
    block_count, slot_count = weight_ref.shape[0], weight_ref.shape[1]
    for block in range(block_count):
        rows = rows_ref[block]
        for slot in range(slot_count):
            part = lax.dot_general(
                weight_ref[block, slot],
                rows,
                (((0,), (0,)), ((), ())),
                preferred_element_type=jnp.float32,
            )
            target = jnp.clip(zone_ref[block, slot] - base_ref[0], 0, 3 * owned - 1)
            group = target // owned
            local = target - group * owned
            for number, table in enumerate(tables):

                @pl.when(group == number)
                def _(table=table, local=local, part=part):
                    table[local] = table[local] + part


def aggregate(block_zone, base, weight_blocks, cell_rows, owned_blocks):
    block_size = weight_blocks.shape[3]
    day_count = cell_rows.shape[2]
    table = jax.ShapeDtypeStruct((owned_blocks, block_size, day_count), jnp.float32)
    return pl.pallas_call(
        aggregate_kernel,
        out_shape=(table, table, table),
        in_specs=[
            pl.BlockSpec(memory_space=pltpu.SMEM),
            pl.BlockSpec(memory_space=pltpu.SMEM),
            pl.BlockSpec(memory_space=pltpu.VMEM),
            pl.BlockSpec(memory_space=pltpu.VMEM),
        ],
        out_specs=(
            pl.BlockSpec(memory_space=pltpu.VMEM),
            pl.BlockSpec(memory_space=pltpu.VMEM),
            pl.BlockSpec(memory_space=pltpu.VMEM),
        ),
    )(block_zone, base, weight_blocks, cell_rows)


def body(runoff, weight_blocks, block_zone, climatology, zone_weight):
    block_count = weight_blocks.shape[0]
    block_size = weight_blocks.shape[2]
    day_count = runoff.shape[1]
    owned_blocks = climatology.shape[0] // block_size
    device_count = lax.axis_size(DEVICE_AXES)
    device_index = lax.axis_index(DEVICE_AXES)
    cell_rows = runoff.reshape(block_count, block_size, day_count)
    base = jnp.reshape((device_index - 1) * owned_blocks, (1,)).astype(jnp.int32)
    to_before, own_table, to_after = aggregate(
        block_zone.astype(jnp.int32), base, weight_blocks, cell_rows, owned_blocks
    )
    from_before = shifted(to_after, DEVICE_AXES, 1)
    from_after = shifted(to_before, DEVICE_AXES, -1)
    summed = own_table + from_before + from_after
    aggregated = summed.reshape(owned_blocks * block_size, day_count)
    anomaly = zone_weight[:, None] * (aggregated - climatology)
    local_gram = jnp.dot(
        anomaly.T, anomaly, precision=exact_mode, preferred_element_type=jnp.float32
    )
    local_gram = 0.5 * (local_gram + local_gram.T)
    total_gram = unpack_gram(all_sum(pack_gram(local_gram), device_count), day_count)
    root = math.sqrt(anomaly.shape[0] * device_count)
    factor, scaled_inverse = cholesky_with_inverse(total_gram, root)
    scores = jnp.dot(anomaly, scaled_inverse.T, precision=exact_mode)
    return (scores, factor)


def solution(mesh):
    return jax.shard_map(
        body,
        mesh=mesh,
        in_specs=(
            P(DEVICE_AXES, None),
            P(DEVICE_AXES, None, None, None),
            P(DEVICE_AXES, None),
            P(DEVICE_AXES, None),
            P(DEVICE_AXES),
        ),
        out_specs=(P(DEVICE_AXES, None), P()),
        check_vma=False,
    )
```

```python
import functools
import itertools
import math

import jax
import jax.numpy as jnp
from jax import lax
from jax.experimental import pallas as pl
from jax.experimental.pallas import tpu as pltpu
from jax.sharding import PartitionSpec as P

exact_mode = lax.Precision.HIGHEST
DEVICE_AXES = ("lat", "sub")
CORE_BIT = 2
PANEL = 64


def shifted(value, axis, steps):
    count = lax.axis_size(axis)
    initial, last = (max(0, -steps), min(count, count - steps))
    return lax.ppermute(value, axis, [(source, source + steps) for source in range(initial, last)])


def exchange_stages(count):
    bits = count.bit_length() - 1
    groups, low = [], 0
    for width in (2, 1, 2, 2):
        if low >= bits:
            break
        if low != CORE_BIT:
            groups.append(list(range(low, min(bits, low + width))))
        low += width
    if low < bits:
        groups.append(list(range(low, bits)))
    return groups


def exchange(value, count, mask):
    return lax.ppermute(value, DEVICE_AXES, [(i, i ^ mask) for i in range(count)])


def all_sum(value, count):
    device_index = lax.axis_index(DEVICE_AXES)
    split = count > (1 << CORE_BIT)
    if split:
        core = (device_index >> CORE_BIT) & 1
        half = value.shape[0] // 2
        low, high = value[:half], value[half:]
        kept = jnp.where(core == 0, low, high)
        sent = jnp.where(core == 0, high, low)
        value = kept + exchange(sent, count, 1 << CORE_BIT)
    for group in exchange_stages(count):
        masks = []
        for size in range(1, len(group) + 1):
            for combo in itertools.combinations(group, size):
                masks.append(sum(1 << bit for bit in combo))
        received = [exchange(value, count, mask) for mask in masks]
        total = received[0]
        for part in received[1:]:
            total = total + part
        value = value + total
    if split:
        other = exchange(value, count, 1 << CORE_BIT)
        value = jnp.where(
            core == 0,
            jnp.concatenate([value, other], axis=0),
            jnp.concatenate([other, value], axis=0),
        )
    return value


def pack_gram(gram):
    half = gram.shape[0] // 2
    rows = lax.broadcasted_iota(jnp.int32, (half, half), 0)
    cols = lax.broadcasted_iota(jnp.int32, (half, half), 1)
    g11, g12, g22 = gram[:half, :half], gram[:half, half:], gram[half:, half:]
    tri = jnp.where(rows <= cols, g11, g22)
    diag = jnp.sum(jnp.where(rows == cols, g22, 0.0), axis=0, keepdims=True)
    extra = jnp.zeros((15, 2 * half), gram.dtype)
    extra_row = jnp.concatenate([diag, jnp.zeros_like(diag)], axis=1)
    return jnp.concatenate([jnp.concatenate([g12, tri], axis=1), extra_row, extra], axis=0)


def unpack_gram(packed, size):
    half = size // 2
    rows = lax.broadcasted_iota(jnp.int32, (half, half), 0)
    cols = lax.broadcasted_iota(jnp.int32, (half, half), 1)
    g12 = packed[:half, :half]
    tri = packed[:half, half:]
    diag = packed[half, :half]
    g11 = jnp.where(rows <= cols, tri, tri.T)
    g22 = jnp.where(rows > cols, tri, jnp.where(rows < cols, tri.T, jnp.diag(diag)))
    top = jnp.concatenate([g11, g12], axis=1)
    bottom = jnp.concatenate([g12.T, g22], axis=1)
    return jnp.concatenate([top, bottom], axis=0)


def cholesky_kernel(gram_ref, upper_ref, inverse_ref, work_ref, *, factor_scale, inverse_scale):
    size = gram_ref.shape[0]
    work_ref[...] = gram_ref[...]
    rows = lax.broadcasted_iota(jnp.int32, (size, size), 0)
    cols = lax.broadcasted_iota(jnp.int32, (size, size), 1)
    inverse_ref[...] = jnp.where(rows == cols, 1.0, 0.0).astype(jnp.float32)
    upper_ref[...] = jnp.zeros((size, size), jnp.float32)
    sub = lax.broadcasted_iota(jnp.int32, (PANEL, 1), 0)
    row_ids = lax.broadcasted_iota(jnp.int32, (size, 1), 0)
    def panel(first, row0, col0, col1):
        lane = lax.broadcasted_iota(jnp.int32, (1, size - col0), 1) + col0
        slab = work_ref[first:first + PANEL, col0:]
        inverse_slab = inverse_ref[first:first + PANEL, :col1]
        upper_slab = jnp.zeros((PANEL, size - col0), jnp.float32)
        for step in range(PANEL):
            column = first + step
            picked = slab[:, column - col0:column - col0 + 1]
            scale = lax.rsqrt(picked[step : step + 1, :])
            upper_row = jnp.where(lane >= column, slab[step : step + 1, :] * scale, 0.0)
            inverse_row = inverse_slab[step : step + 1, :] * scale
            coef = jnp.where(sub > step, picked * scale, 0.0)
            slab = slab - coef * upper_row
            inverse_slab = jnp.where(sub == step, inverse_row, inverse_slab - coef * inverse_row)
            upper_slab = jnp.where(sub == step, upper_row, upper_slab)
        upper_ref[first:first + PANEL, col0:] = upper_slab * factor_scale
        inverse_ref[first:first + PANEL, :col1] = inverse_slab * inverse_scale
        lower_cols = jnp.transpose(upper_slab)[row0 - col0:]
        lower_cols = jnp.where(row_ids[row0:] >= first + PANEL, lower_cols, 0.0)
        work_ref[row0:, col0:] = work_ref[row0:, col0:] - jnp.dot(
            lower_cols, upper_slab, precision=exact_mode, preferred_element_type=jnp.float32)
        inverse_ref[row0:, :col1] = inverse_ref[row0:, :col1] - jnp.dot(
            lower_cols, inverse_slab, precision=exact_mode, preferred_element_type=jnp.float32)

    quarter = size // 4
    for part in range(4):
        row0 = quarter * part
        col0 = (size // 2) * (part // 2)
        col1 = (size // 2) * (part // 2 + 1)
        for first in range(row0, row0 + quarter, PANEL):
            panel(first, row0, col0, col1)


def cholesky_with_inverse(gram, root):
    size = gram.shape[0]
    return pl.pallas_call(
        functools.partial(cholesky_kernel, factor_scale=1.0 / root, inverse_scale=root),
        out_shape=(
            jax.ShapeDtypeStruct((size, size), jnp.float32),
            jax.ShapeDtypeStruct((size, size), jnp.float32),
        ),
        scratch_shapes=[pltpu.VMEM((size, size), jnp.float32)],
    )(gram)


def aggregate_kernel(zone_ref, base_ref, weight_ref, rows_ref, before_ref, own_ref, after_ref, work_ref):
    owned = own_ref.shape[0]
    work_ref[...] = jnp.zeros(work_ref.shape, work_ref.dtype)
    block_count, slot_count = weight_ref.shape[0], weight_ref.shape[1]
    for block in range(block_count):
        rows = rows_ref[block]
        for slot in range(slot_count):
            part = lax.dot_general(
                weight_ref[block, slot],
                rows,
                (((0,), (0,)), ((), ())),
                preferred_element_type=jnp.float32,
            )
            target = jnp.clip(zone_ref[block, slot] - base_ref[0], 0, 3 * owned - 1)
            work_ref[target] = work_ref[target] + part
    before_ref[...] = work_ref[:owned]
    own_ref[...] = work_ref[owned : 2 * owned]
    after_ref[...] = work_ref[2 * owned :]


def aggregate(block_zone, base, weight_blocks, cell_rows, owned_blocks):
    block_size = weight_blocks.shape[3]
    day_count = cell_rows.shape[2]
    table = jax.ShapeDtypeStruct((owned_blocks, block_size, day_count), jnp.float32)
    return pl.pallas_call(
        aggregate_kernel,
        out_shape=(table, table, table),
        in_specs=[
            pl.BlockSpec(memory_space=pltpu.SMEM),
            pl.BlockSpec(memory_space=pltpu.SMEM),
            pl.BlockSpec(memory_space=pltpu.VMEM),
            pl.BlockSpec(memory_space=pltpu.VMEM),
        ],
        out_specs=(
            pl.BlockSpec(memory_space=pltpu.VMEM),
            pl.BlockSpec(memory_space=pltpu.VMEM),
            pl.BlockSpec(memory_space=pltpu.VMEM),
        ),
        scratch_shapes=[pltpu.VMEM((3 * owned_blocks, block_size, day_count), jnp.float32)],
    )(block_zone, base, weight_blocks, cell_rows)


def body(runoff, weight_blocks, block_zone, climatology, zone_weight):
    block_count = weight_blocks.shape[0]
    block_size = weight_blocks.shape[2]
    day_count = runoff.shape[1]
    owned_blocks = climatology.shape[0] // block_size
    device_count = lax.axis_size(DEVICE_AXES)
    device_index = lax.axis_index(DEVICE_AXES)
    cell_rows = runoff.reshape(block_count, block_size, day_count)
    base = jnp.reshape((device_index - 1) * owned_blocks, (1,)).astype(jnp.int32)
    to_before, own_table, to_after = aggregate(
        block_zone.astype(jnp.int32), base, weight_blocks, cell_rows, owned_blocks
    )
    from_before = shifted(to_after, DEVICE_AXES, 1)
    from_after = shifted(to_before, DEVICE_AXES, -1)
    summed = own_table + from_before + from_after
    aggregated = summed.reshape(owned_blocks * block_size, day_count)
    anomaly = zone_weight[:, None] * (aggregated - climatology)
    local_gram = jnp.dot(
        anomaly.T, anomaly, precision=exact_mode, preferred_element_type=jnp.float32
    )
    local_gram = 0.5 * (local_gram + local_gram.T)
    total_gram = unpack_gram(all_sum(pack_gram(local_gram), device_count), day_count)
    root = math.sqrt(anomaly.shape[0] * device_count)
    factor, scaled_inverse = cholesky_with_inverse(total_gram, root)
    scores = jnp.dot(anomaly, scaled_inverse.T, precision=exact_mode)
    return (scores, factor)


def solution(mesh):
    return jax.shard_map(
        body,
        mesh=mesh,
        in_specs=(
            P(DEVICE_AXES, None),
            P(DEVICE_AXES, None, None, None),
            P(DEVICE_AXES, None),
            P(DEVICE_AXES, None),
            P(DEVICE_AXES),
        ),
        out_specs=(P(DEVICE_AXES, None), P()),
        check_vma=False,
    )
```

```python
import functools
import itertools
import math

import jax
import jax.numpy as jnp
from jax import lax
from jax.experimental import pallas as pl
from jax.experimental.pallas import tpu as pltpu
from jax.sharding import PartitionSpec as P

exact_mode = lax.Precision.HIGHEST
DEVICE_AXES = ("lat", "sub")
CORE_BIT = 2
PANEL = 64


def shifted(value, axis, steps):
    count = lax.axis_size(axis)
    initial, last = (max(0, -steps), min(count, count - steps))
    return lax.ppermute(value, axis, [(source, source + steps) for source in range(initial, last)])


def exchange_stages(count):
    bits = count.bit_length() - 1
    groups, low = [], 0
    for width in (2, 1, 2, 2):
        if low >= bits:
            break
        if low != CORE_BIT:
            groups.append(list(range(low, min(bits, low + width))))
        low += width
    if low < bits:
        groups.append(list(range(low, bits)))
    return groups


def exchange(value, count, mask):
    return lax.ppermute(value, DEVICE_AXES, [(i, i ^ mask) for i in range(count)])


def all_sum(value, count):
    device_index = lax.axis_index(DEVICE_AXES)
    split = count > (1 << CORE_BIT)
    if split:
        core = (device_index >> CORE_BIT) & 1
        half = value.shape[0] // 2
        low, high = value[:half], value[half:]
        kept = jnp.where(core == 0, low, high)
        sent = jnp.where(core == 0, high, low)
        value = kept + exchange(sent, count, 1 << CORE_BIT)
    for group in exchange_stages(count):
        masks = []
        for size in range(1, len(group) + 1):
            for combo in itertools.combinations(group, size):
                masks.append(sum(1 << bit for bit in combo))
        received = [exchange(value, count, mask) for mask in masks]
        total = received[0]
        for part in received[1:]:
            total = total + part
        value = value + total
    if split:
        other = exchange(value, count, 1 << CORE_BIT)
        value = jnp.where(
            core == 0,
            jnp.concatenate([value, other], axis=0),
            jnp.concatenate([other, value], axis=0),
        )
    return value


def pack_gram(gram):
    half = gram.shape[0] // 2
    rows = lax.broadcasted_iota(jnp.int32, (half, half), 0)
    cols = lax.broadcasted_iota(jnp.int32, (half, half), 1)
    g11, g12, g22 = gram[:half, :half], gram[:half, half:], gram[half:, half:]
    tri = jnp.where(rows <= cols, g11, g22)
    diag = jnp.sum(jnp.where(rows == cols, g22, 0.0), axis=0, keepdims=True)
    extra = jnp.zeros((15, 2 * half), gram.dtype)
    extra_row = jnp.concatenate([diag, jnp.zeros_like(diag)], axis=1)
    return jnp.concatenate([jnp.concatenate([g12, tri], axis=1), extra_row, extra], axis=0)


def unpack_gram(packed, size):
    half = size // 2
    rows = lax.broadcasted_iota(jnp.int32, (half, half), 0)
    cols = lax.broadcasted_iota(jnp.int32, (half, half), 1)
    g12 = packed[:half, :half]
    tri = packed[:half, half:]
    diag = packed[half, :half]
    g11 = jnp.where(rows <= cols, tri, tri.T)
    g22 = jnp.where(rows > cols, tri, jnp.where(rows < cols, tri.T, jnp.diag(diag)))
    top = jnp.concatenate([g11, g12], axis=1)
    bottom = jnp.concatenate([g12.T, g22], axis=1)
    return jnp.concatenate([top, bottom], axis=0)


def cholesky_kernel(gram_ref, upper_ref, inverse_ref, work_ref, *, factor_scale, inverse_scale):
    size = gram_ref.shape[0]
    work_ref[...] = gram_ref[...]
    rows = lax.broadcasted_iota(jnp.int32, (size, size), 0)
    cols = lax.broadcasted_iota(jnp.int32, (size, size), 1)
    inverse_ref[...] = jnp.where(rows == cols, 1.0, 0.0).astype(jnp.float32)
    upper_ref[...] = jnp.zeros((size, size), jnp.float32)
    sub = lax.broadcasted_iota(jnp.int32, (PANEL, 1), 0)
    row_ids = lax.broadcasted_iota(jnp.int32, (size, 1), 0)
    def panel(first, row0, col0, col1):
        lane = lax.broadcasted_iota(jnp.int32, (1, size - col0), 1) + col0
        slab = work_ref[first:first + PANEL, col0:]
        inverse_slab = inverse_ref[first:first + PANEL, :col1]
        upper_slab = jnp.zeros((PANEL, size - col0), jnp.float32)
        for step in range(PANEL):
            column = first + step
            picked = slab[:, column - col0:column - col0 + 1]
            scale = lax.rsqrt(picked[step : step + 1, :])
            upper_row = jnp.where(lane >= column, slab[step : step + 1, :] * scale, 0.0)
            inverse_row = inverse_slab[step : step + 1, :] * scale
            coef = jnp.where(sub > step, picked * scale, 0.0)
            slab = slab - coef * upper_row
            inverse_slab = jnp.where(sub == step, inverse_row, inverse_slab - coef * inverse_row)
            upper_slab = jnp.where(sub == step, upper_row, upper_slab)
        upper_ref[first:first + PANEL, col0:] = upper_slab * factor_scale
        inverse_ref[first:first + PANEL, :col1] = inverse_slab * inverse_scale
        lower_cols = jnp.transpose(upper_slab)[row0 - col0:]
        lower_cols = jnp.where(row_ids[row0:] >= first + PANEL, lower_cols, 0.0)
        work_ref[row0:, col0:] = work_ref[row0:, col0:] - jnp.dot(
            lower_cols, upper_slab, precision=exact_mode, preferred_element_type=jnp.float32)
        inverse_ref[row0:, :col1] = inverse_ref[row0:, :col1] - jnp.dot(
            lower_cols, inverse_slab, precision=exact_mode, preferred_element_type=jnp.float32)

    quarter = size // 4
    for part in range(4):
        row0 = quarter * part
        col0 = (size // 2) * (part // 2)
        col1 = (size // 2) * (part // 2 + 1)
        for first in range(row0, row0 + quarter, PANEL):
            panel(first, row0, col0, col1)


def cholesky_with_inverse(gram, root):
    size = gram.shape[0]
    return pl.pallas_call(
        functools.partial(cholesky_kernel, factor_scale=1.0 / root, inverse_scale=root),
        out_shape=(
            jax.ShapeDtypeStruct((size, size), jnp.float32),
            jax.ShapeDtypeStruct((size, size), jnp.float32),
        ),
        scratch_shapes=[pltpu.VMEM((size, size), jnp.float32)],
    )(gram)


def aggregate_kernel(zone_ref, base_ref, weight_ref, rows_ref, before_ref, own_ref, after_ref, work_ref):
    owned = own_ref.shape[0]
    work_ref[...] = jnp.zeros(work_ref.shape, work_ref.dtype)
    block_count, slot_count = weight_ref.shape[0], weight_ref.shape[1]
    for block in range(block_count):
        rows = rows_ref[block]
        for slot in range(slot_count):
            part = lax.dot_general(
                weight_ref[block, slot],
                rows,
                (((0,), (0,)), ((), ())),
                preferred_element_type=jnp.float32,
            )
            target = jnp.clip(zone_ref[block, slot] - base_ref[0], 0, 3 * owned - 1)
            work_ref[target] = work_ref[target] + part
    before_ref[...] = work_ref[:owned]
    own_ref[...] = work_ref[owned : 2 * owned]
    after_ref[...] = work_ref[2 * owned :]


def aggregate(block_zone, base, weight_blocks, cell_rows, owned_blocks):
    block_size = weight_blocks.shape[3]
    day_count = cell_rows.shape[2]
    table = jax.ShapeDtypeStruct((owned_blocks, block_size, day_count), jnp.float32)
    return pl.pallas_call(
        aggregate_kernel,
        out_shape=(table, table, table),
        in_specs=[
            pl.BlockSpec(memory_space=pltpu.SMEM),
            pl.BlockSpec(memory_space=pltpu.SMEM),
            pl.BlockSpec(memory_space=pltpu.VMEM),
            pl.BlockSpec(memory_space=pltpu.VMEM),
        ],
        out_specs=(
            pl.BlockSpec(memory_space=pltpu.VMEM),
            pl.BlockSpec(memory_space=pltpu.VMEM),
            pl.BlockSpec(memory_space=pltpu.VMEM),
        ),
        scratch_shapes=[pltpu.VMEM((3 * owned_blocks, block_size, day_count), jnp.float32)],
    )(block_zone, base, weight_blocks, cell_rows)


def body(runoff, weight_blocks, block_zone, climatology, zone_weight):
    block_count = weight_blocks.shape[0]
    block_size = weight_blocks.shape[2]
    day_count = runoff.shape[1]
    owned_blocks = climatology.shape[0] // block_size
    device_count = lax.axis_size(DEVICE_AXES)
    device_index = lax.axis_index(DEVICE_AXES)
    cell_rows = runoff.reshape(block_count, block_size, day_count)
    base = jnp.reshape((device_index - 1) * owned_blocks, (1,)).astype(jnp.int32)
    to_before, own_table, to_after = aggregate(
        block_zone.astype(jnp.int32), base, weight_blocks, cell_rows, owned_blocks
    )
    from_before = shifted(to_after, DEVICE_AXES, 1)
    from_after = shifted(to_before, DEVICE_AXES, -1)
    summed = own_table + from_before + from_after
    aggregated = summed.reshape(owned_blocks * block_size, day_count)
    anomaly = zone_weight[:, None] * (aggregated - climatology)
    local_gram = jnp.dot(
        anomaly.T, anomaly, precision=exact_mode, preferred_element_type=jnp.float32
    )
    local_gram = 0.5 * (local_gram + local_gram.T)
    total_gram = unpack_gram(all_sum(pack_gram(local_gram), device_count), day_count)
    root = math.sqrt(anomaly.shape[0] * device_count)
    factor, scaled_inverse = cholesky_with_inverse(total_gram, root)
    scores = jnp.dot(anomaly, scaled_inverse.T, precision=lax.Precision.HIGH)
    return (scores, factor)


def solution(mesh):
    return jax.shard_map(
        body,
        mesh=mesh,
        in_specs=(
            P(DEVICE_AXES, None),
            P(DEVICE_AXES, None, None, None),
            P(DEVICE_AXES, None),
            P(DEVICE_AXES, None),
            P(DEVICE_AXES),
        ),
        out_specs=(P(DEVICE_AXES, None), P()),
        check_vma=False,
    )
```

```python
import functools
import itertools
import math

import jax
import jax.numpy as jnp
from jax import lax
from jax.experimental import pallas as pl
from jax.experimental.pallas import tpu as pltpu
from jax.sharding import PartitionSpec as P

exact_mode = lax.Precision.HIGHEST
DEVICE_AXES = ("lat", "sub")
CORE_BIT = 2
PANEL = 64


def shifted(value, axis, steps):
    count = lax.axis_size(axis)
    initial, last = (max(0, -steps), min(count, count - steps))
    return lax.ppermute(value, axis, [(source, source + steps) for source in range(initial, last)])


def exchange_stages(count):
    bits = count.bit_length() - 1
    groups, low = [], 0
    for width in (2, 1, 2, 2):
        if low >= bits:
            break
        if low != CORE_BIT:
            groups.append(list(range(low, min(bits, low + width))))
        low += width
    if low < bits:
        groups.append(list(range(low, bits)))
    return groups


def exchange(value, count, mask):
    return lax.ppermute(value, DEVICE_AXES, [(i, i ^ mask) for i in range(count)])


def all_sum(value, count):
    device_index = lax.axis_index(DEVICE_AXES)
    split = count > (1 << CORE_BIT)
    if split:
        core = (device_index >> CORE_BIT) & 1
        half = value.shape[0] // 2
        low, high = value[:half], value[half:]
        kept = jnp.where(core == 0, low, high)
        sent = jnp.where(core == 0, high, low)
        value = kept + exchange(sent, count, 1 << CORE_BIT)
    for group in exchange_stages(count):
        masks = []
        for size in range(1, len(group) + 1):
            for combo in itertools.combinations(group, size):
                masks.append(sum(1 << bit for bit in combo))
        received = [exchange(value, count, mask) for mask in masks]
        total = received[0]
        for part in received[1:]:
            total = total + part
        value = value + total
    if split:
        other = exchange(value, count, 1 << CORE_BIT)
        value = jnp.where(
            core == 0,
            jnp.concatenate([value, other], axis=0),
            jnp.concatenate([other, value], axis=0),
        )
    return value


def pack_gram(gram):
    half = gram.shape[0] // 2
    rows = lax.broadcasted_iota(jnp.int32, (half, half), 0)
    cols = lax.broadcasted_iota(jnp.int32, (half, half), 1)
    g11, g12, g22 = gram[:half, :half], gram[:half, half:], gram[half:, half:]
    tri = jnp.where(rows <= cols, g11, g22)
    diag = jnp.sum(jnp.where(rows == cols, g22, 0.0), axis=0, keepdims=True)
    extra = jnp.zeros((15, 2 * half), gram.dtype)
    extra_row = jnp.concatenate([diag, jnp.zeros_like(diag)], axis=1)
    return jnp.concatenate([jnp.concatenate([g12, tri], axis=1), extra_row, extra], axis=0)


def unpack_gram(packed, size):
    half = size // 2
    rows = lax.broadcasted_iota(jnp.int32, (half, half), 0)
    cols = lax.broadcasted_iota(jnp.int32, (half, half), 1)
    g12 = packed[:half, :half]
    tri = packed[:half, half:]
    diag = packed[half, :half]
    g11 = jnp.where(rows <= cols, tri, tri.T)
    g22 = jnp.where(rows > cols, tri, jnp.where(rows < cols, tri.T, jnp.diag(diag)))
    top = jnp.concatenate([g11, g12], axis=1)
    bottom = jnp.concatenate([g12.T, g22], axis=1)
    return jnp.concatenate([top, bottom], axis=0)


def cholesky_kernel(gram_ref, anomaly_ref, upper_ref, scores_ref, inverse_ref, work_ref, *, factor_scale, inverse_scale):
    size = gram_ref.shape[0]
    work_ref[...] = gram_ref[...]
    rows = lax.broadcasted_iota(jnp.int32, (size, size), 0)
    cols = lax.broadcasted_iota(jnp.int32, (size, size), 1)
    inverse_ref[...] = jnp.where(rows == cols, 1.0, 0.0).astype(jnp.float32)
    upper_ref[...] = jnp.zeros((size, size), jnp.float32)
    sub = lax.broadcasted_iota(jnp.int32, (PANEL, 1), 0)
    row_ids = lax.broadcasted_iota(jnp.int32, (size, 1), 0)
    def panel(first, row0, col0, col1):
        lane = lax.broadcasted_iota(jnp.int32, (1, size - col0), 1) + col0
        slab = work_ref[first:first + PANEL, col0:]
        inverse_slab = inverse_ref[first:first + PANEL, :col1]
        upper_slab = jnp.zeros((PANEL, size - col0), jnp.float32)
        for step in range(PANEL):
            column = first + step
            picked = slab[:, column - col0:column - col0 + 1]
            scale = lax.rsqrt(picked[step : step + 1, :])
            upper_row = jnp.where(lane >= column, slab[step : step + 1, :] * scale, 0.0)
            inverse_row = inverse_slab[step : step + 1, :] * scale
            coef = jnp.where(sub > step, picked * scale, 0.0)
            slab = slab - coef * upper_row
            inverse_slab = jnp.where(sub == step, inverse_row, inverse_slab - coef * inverse_row)
            upper_slab = jnp.where(sub == step, upper_row, upper_slab)
        upper_ref[first:first + PANEL, col0:] = upper_slab * factor_scale
        inverse_ref[first:first + PANEL, :col1] = inverse_slab * inverse_scale
        lower_cols = jnp.transpose(upper_slab)[row0 - col0:]
        lower_cols = jnp.where(row_ids[row0:] >= first + PANEL, lower_cols, 0.0)
        work_ref[row0:, col0:] = work_ref[row0:, col0:] - jnp.dot(
            lower_cols, upper_slab, precision=exact_mode, preferred_element_type=jnp.float32)
        inverse_ref[row0:, :col1] = inverse_ref[row0:, :col1] - jnp.dot(
            lower_cols, inverse_slab, precision=exact_mode, preferred_element_type=jnp.float32)

    quarter = size // 4
    for part in range(4):
        row0 = quarter * part
        col0 = (size // 2) * (part // 2)
        col1 = (size // 2) * (part // 2 + 1)
        for first in range(row0, row0 + quarter, PANEL):
            panel(first, row0, col0, col1)
    scores_ref[...] = lax.dot_general(
        anomaly_ref[...], inverse_ref[...], (((1,), (1,)), ((), ())),
        precision=exact_mode, preferred_element_type=jnp.float32,
    )


def cholesky_with_inverse(gram, anomaly, root):
    size = gram.shape[0]
    square = jax.ShapeDtypeStruct((size, size), jnp.float32)
    return pl.pallas_call(
        functools.partial(cholesky_kernel, factor_scale=1.0 / root, inverse_scale=root),
        out_shape=(square, jax.ShapeDtypeStruct(anomaly.shape, jnp.float32)),
        scratch_shapes=[pltpu.VMEM((size, size), jnp.float32), pltpu.VMEM((size, size), jnp.float32)],
    )(gram, anomaly)


def aggregate_kernel(zone_ref, base_ref, weight_ref, rows_ref, before_ref, own_ref, after_ref, work_ref):
    owned = own_ref.shape[0]
    work_ref[...] = jnp.zeros(work_ref.shape, work_ref.dtype)
    block_count, slot_count = weight_ref.shape[0], weight_ref.shape[1]
    for block in range(block_count):
        rows = rows_ref[block]
        for slot in range(slot_count):
            part = lax.dot_general(
                weight_ref[block, slot],
                rows,
                (((0,), (0,)), ((), ())),
                preferred_element_type=jnp.float32,
            )
            target = jnp.clip(zone_ref[block, slot] - base_ref[0], 0, 3 * owned - 1)
            work_ref[target] = work_ref[target] + part
    before_ref[...] = work_ref[:owned]
    own_ref[...] = work_ref[owned : 2 * owned]
    after_ref[...] = work_ref[2 * owned :]


def aggregate(block_zone, base, weight_blocks, cell_rows, owned_blocks):
    block_size = weight_blocks.shape[3]
    day_count = cell_rows.shape[2]
    table = jax.ShapeDtypeStruct((owned_blocks, block_size, day_count), jnp.float32)
    return pl.pallas_call(
        aggregate_kernel,
        out_shape=(table, table, table),
        in_specs=[
            pl.BlockSpec(memory_space=pltpu.SMEM),
            pl.BlockSpec(memory_space=pltpu.SMEM),
            pl.BlockSpec(memory_space=pltpu.VMEM),
            pl.BlockSpec(memory_space=pltpu.VMEM),
        ],
        out_specs=(
            pl.BlockSpec(memory_space=pltpu.VMEM),
            pl.BlockSpec(memory_space=pltpu.VMEM),
            pl.BlockSpec(memory_space=pltpu.VMEM),
        ),
        scratch_shapes=[pltpu.VMEM((3 * owned_blocks, block_size, day_count), jnp.float32)],
    )(block_zone, base, weight_blocks, cell_rows)


def body(runoff, weight_blocks, block_zone, climatology, zone_weight):
    block_count = weight_blocks.shape[0]
    block_size = weight_blocks.shape[2]
    day_count = runoff.shape[1]
    owned_blocks = climatology.shape[0] // block_size
    device_count = lax.axis_size(DEVICE_AXES)
    device_index = lax.axis_index(DEVICE_AXES)
    cell_rows = runoff.reshape(block_count, block_size, day_count)
    base = jnp.reshape((device_index - 1) * owned_blocks, (1,)).astype(jnp.int32)
    to_before, own_table, to_after = aggregate(
        block_zone.astype(jnp.int32), base, weight_blocks, cell_rows, owned_blocks
    )
    from_before = shifted(to_after, DEVICE_AXES, 1)
    from_after = shifted(to_before, DEVICE_AXES, -1)
    summed = own_table + from_before + from_after
    aggregated = summed.reshape(owned_blocks * block_size, day_count)
    anomaly = zone_weight[:, None] * (aggregated - climatology)
    local_gram = jnp.dot(
        anomaly.T, anomaly, precision=exact_mode, preferred_element_type=jnp.float32
    )
    local_gram = 0.5 * (local_gram + local_gram.T)
    total_gram = unpack_gram(all_sum(pack_gram(local_gram), device_count), day_count)
    root = math.sqrt(anomaly.shape[0] * device_count)
    factor, scores = cholesky_with_inverse(total_gram, anomaly, root)
    return (scores, factor)


def solution(mesh):
    return jax.shard_map(
        body,
        mesh=mesh,
        in_specs=(
            P(DEVICE_AXES, None),
            P(DEVICE_AXES, None, None, None),
            P(DEVICE_AXES, None),
            P(DEVICE_AXES, None),
            P(DEVICE_AXES),
        ),
        out_specs=(P(DEVICE_AXES, None), P()),
        check_vma=False,
    )
```

```python
import functools
import itertools
import math

import jax
import jax.numpy as jnp
from jax import lax
from jax.experimental import pallas as pl
from jax.experimental.pallas import tpu as pltpu
from jax.sharding import PartitionSpec as P

exact_mode = lax.Precision.HIGHEST
DEVICE_AXES = ("lat", "sub")
CORE_BIT = 2
PANEL = 64


def shifted(value, axis, steps):
    count = lax.axis_size(axis)
    initial, last = (max(0, -steps), min(count, count - steps))
    return lax.ppermute(value, axis, [(source, source + steps) for source in range(initial, last)])


def exchange_stages(count):
    bits = count.bit_length() - 1
    groups, low = [], 0
    for width in (2, 1, 2, 2):
        if low >= bits:
            break
        if low != CORE_BIT:
            groups.append(list(range(low, min(bits, low + width))))
        low += width
    if low < bits:
        groups.append(list(range(low, bits)))
    return groups


def exchange(value, count, mask):
    return lax.ppermute(value, DEVICE_AXES, [(i, i ^ mask) for i in range(count)])


def all_sum(value, count):
    device_index = lax.axis_index(DEVICE_AXES)
    split = count > (1 << CORE_BIT)
    if split:
        core = (device_index >> CORE_BIT) & 1
        half = value.shape[0] // 2
        low, high = value[:half], value[half:]
        kept = jnp.where(core == 0, low, high)
        sent = jnp.where(core == 0, high, low)
        value = kept + exchange(sent, count, 1 << CORE_BIT)
    for group in exchange_stages(count):
        masks = []
        for size in range(1, len(group) + 1):
            for combo in itertools.combinations(group, size):
                masks.append(sum(1 << bit for bit in combo))
        received = [exchange(value, count, mask) for mask in masks]
        total = received[0]
        for part in received[1:]:
            total = total + part
        value = value + total
    if split:
        other = exchange(value, count, 1 << CORE_BIT)
        value = jnp.where(
            core == 0,
            jnp.concatenate([value, other], axis=0),
            jnp.concatenate([other, value], axis=0),
        )
    return value


def pack_gram(gram):
    half = gram.shape[0] // 2
    rows = lax.broadcasted_iota(jnp.int32, (half, half), 0)
    cols = lax.broadcasted_iota(jnp.int32, (half, half), 1)
    g11, g12, g22 = gram[:half, :half], gram[:half, half:], gram[half:, half:]
    tri = jnp.where(rows <= cols, g11, g22)
    diag = jnp.sum(jnp.where(rows == cols, g22, 0.0), axis=0, keepdims=True)
    extra = jnp.zeros((15, 2 * half), gram.dtype)
    extra_row = jnp.concatenate([diag, jnp.zeros_like(diag)], axis=1)
    return jnp.concatenate([jnp.concatenate([g12, tri], axis=1), extra_row, extra], axis=0)


def unpack_gram(packed, size):
    half = size // 2
    rows = lax.broadcasted_iota(jnp.int32, (half, half), 0)
    cols = lax.broadcasted_iota(jnp.int32, (half, half), 1)
    g12 = packed[:half, :half]
    tri = packed[:half, half:]
    diag = packed[half, :half]
    g11 = jnp.where(rows <= cols, tri, tri.T)
    g22 = jnp.where(rows > cols, tri, jnp.where(rows < cols, tri.T, jnp.diag(diag)))
    top = jnp.concatenate([g11, g12], axis=1)
    bottom = jnp.concatenate([g12.T, g22], axis=1)
    return jnp.concatenate([top, bottom], axis=0)


def cholesky_kernel(gram_ref, anomaly_ref, upper_ref, scores_ref, inverse_ref, work_ref, *, factor_scale, inverse_scale):
    size = gram_ref.shape[0]
    work_ref[...] = gram_ref[...]
    rows = lax.broadcasted_iota(jnp.int32, (size, size), 0)
    cols = lax.broadcasted_iota(jnp.int32, (size, size), 1)
    inverse_ref[...] = jnp.where(rows == cols, 1.0, 0.0).astype(jnp.float32)
    upper_ref[...] = jnp.zeros((size, size), jnp.float32)
    sub = lax.broadcasted_iota(jnp.int32, (PANEL, 1), 0)
    row_ids = lax.broadcasted_iota(jnp.int32, (size, 1), 0)
    def panel(first, row0, col0, col1):
        lane = lax.broadcasted_iota(jnp.int32, (1, size - col0), 1) + col0
        slab = work_ref[first:first + PANEL, col0:]
        inverse_slab = inverse_ref[first:first + PANEL, :col1]
        upper_slab = jnp.zeros((PANEL, size - col0), jnp.float32)
        for step in range(PANEL):
            column = first + step
            picked = slab[:, column - col0:column - col0 + 1]
            scale = lax.rsqrt(picked[step : step + 1, :])
            upper_row = jnp.where(lane >= column, slab[step : step + 1, :] * scale, 0.0)
            inverse_row = inverse_slab[step : step + 1, :] * scale
            coef = jnp.where(sub > step, picked * scale, 0.0)
            slab = slab - coef * upper_row
            inverse_slab = jnp.where(sub == step, inverse_row, inverse_slab - coef * inverse_row)
            upper_slab = jnp.where(sub == step, upper_row, upper_slab)
        upper_ref[first:first + PANEL, col0:] = upper_slab * factor_scale
        inverse_ref[first:first + PANEL, :col1] = inverse_slab * inverse_scale
        lower_cols = jnp.transpose(upper_slab)[row0 - col0:]
        lower_cols = jnp.where(row_ids[row0:] >= first + PANEL, lower_cols, 0.0)
        work_ref[row0:, col0:] = work_ref[row0:, col0:] - jnp.dot(
            lower_cols, upper_slab, precision=exact_mode, preferred_element_type=jnp.float32)
        inverse_ref[row0:, :col1] = inverse_ref[row0:, :col1] - jnp.dot(
            lower_cols, inverse_slab, precision=exact_mode, preferred_element_type=jnp.float32)

    quarter = size // 4
    for part in range(4):
        row0 = quarter * part
        col0 = (size // 2) * (part // 2)
        col1 = (size // 2) * (part // 2 + 1)
        for first in range(row0, row0 + quarter, PANEL):
            panel(first, row0, col0, col1)
    scores_ref[...] = lax.dot_general(
        anomaly_ref[...], inverse_ref[...], (((1,), (1,)), ((), ())),
        precision=exact_mode, preferred_element_type=jnp.float32,
    )


def cholesky_with_inverse(gram, anomaly, root):
    size = gram.shape[0]
    square = jax.ShapeDtypeStruct((size, size), jnp.float32)
    return pl.pallas_call(
        functools.partial(cholesky_kernel, factor_scale=1.0 / root, inverse_scale=root),
        out_shape=(square, jax.ShapeDtypeStruct(anomaly.shape, jnp.float32)),
        scratch_shapes=[pltpu.VMEM((size, size), jnp.float32), pltpu.VMEM((size, size), jnp.float32)],
    )(gram, anomaly)


def aggregate_kernel(zone_ref, base_ref, weight_ref, rows_ref, before_ref, own_ref, after_ref, work_ref):
    owned = own_ref.shape[0]
    work_ref[...] = jnp.zeros(work_ref.shape, work_ref.dtype)
    block_count, slot_count = weight_ref.shape[0], weight_ref.shape[1]
    for block in range(block_count):
        rows = rows_ref[block]
        for slot in range(slot_count):
            part = lax.dot_general(
                weight_ref[block, slot],
                rows,
                (((0,), (0,)), ((), ())),
                preferred_element_type=jnp.float32,
            )
            target = jnp.clip(zone_ref[slot, block] - base_ref[0], 0, 3 * owned - 1)
            work_ref[target] = work_ref[target] + part
    before_ref[...] = work_ref[:owned]
    own_ref[...] = work_ref[owned : 2 * owned]
    after_ref[...] = work_ref[2 * owned :]


def aggregate(zone_by_slot, base, weight_blocks, cell_rows, owned_blocks):
    block_size = weight_blocks.shape[3]
    day_count = cell_rows.shape[2]
    table = jax.ShapeDtypeStruct((owned_blocks, block_size, day_count), jnp.float32)
    return pl.pallas_call(
        aggregate_kernel,
        out_shape=(table, table, table),
        in_specs=[
            pl.BlockSpec(memory_space=pltpu.SMEM),
            pl.BlockSpec(memory_space=pltpu.SMEM),
            pl.BlockSpec(memory_space=pltpu.VMEM),
            pl.BlockSpec(memory_space=pltpu.VMEM),
        ],
        out_specs=(
            pl.BlockSpec(memory_space=pltpu.VMEM),
            pl.BlockSpec(memory_space=pltpu.VMEM),
            pl.BlockSpec(memory_space=pltpu.VMEM),
        ),
        scratch_shapes=[pltpu.VMEM((3 * owned_blocks, block_size, day_count), jnp.float32)],
    )(zone_by_slot, base, weight_blocks, cell_rows)


def body(runoff, weight_blocks, block_zone, climatology, zone_weight):
    block_count = weight_blocks.shape[0]
    block_size = weight_blocks.shape[2]
    day_count = runoff.shape[1]
    owned_blocks = climatology.shape[0] // block_size
    device_count = lax.axis_size(DEVICE_AXES)
    device_index = lax.axis_index(DEVICE_AXES)
    cell_rows = runoff.reshape(block_count, block_size, day_count)
    base = jnp.reshape((device_index - 1) * owned_blocks, (1,)).astype(jnp.int32)
    to_before, own_table, to_after = aggregate(
        block_zone.astype(jnp.int32).T, base, weight_blocks, cell_rows, owned_blocks
    )
    from_before = shifted(to_after, DEVICE_AXES, 1)
    from_after = shifted(to_before, DEVICE_AXES, -1)
    summed = own_table + from_before + from_after
    aggregated = summed.reshape(owned_blocks * block_size, day_count)
    anomaly = zone_weight[:, None] * (aggregated - climatology)
    local_gram = jnp.dot(
        anomaly.T, anomaly, precision=exact_mode, preferred_element_type=jnp.float32
    )
    local_gram = 0.5 * (local_gram + local_gram.T)
    total_gram = unpack_gram(all_sum(pack_gram(local_gram), device_count), day_count)
    root = math.sqrt(anomaly.shape[0] * device_count)
    factor, scores = cholesky_with_inverse(total_gram, anomaly, root)
    return (scores, factor)


def solution(mesh):
    return jax.shard_map(
        body,
        mesh=mesh,
        in_specs=(
            P(DEVICE_AXES, None),
            P(DEVICE_AXES, None, None, None),
            P(DEVICE_AXES, None),
            P(DEVICE_AXES, None),
            P(DEVICE_AXES),
        ),
        out_specs=(P(DEVICE_AXES, None), P()),
        check_vma=False,
    )
```

```python
import functools
import itertools
import math

import jax
import jax.numpy as jnp
from jax import lax
from jax.experimental import pallas as pl
from jax.experimental.pallas import tpu as pltpu
from jax.sharding import PartitionSpec as P

exact_mode = lax.Precision.HIGHEST
DEVICE_AXES = ("lat", "sub")
CORE_BIT = 2
PANEL = 64


def shifted(value, axis, steps):
    count = lax.axis_size(axis)
    initial, last = (max(0, -steps), min(count, count - steps))
    return lax.ppermute(value, axis, [(source, source + steps) for source in range(initial, last)])


def exchange_stages(count):
    bits = count.bit_length() - 1
    groups, low = [], 0
    for width in (2, 1, 2, 2):
        if low >= bits:
            break
        if low != CORE_BIT:
            groups.append(list(range(low, min(bits, low + width))))
        low += width
    if low < bits:
        groups.append(list(range(low, bits)))
    return groups


def exchange(value, count, mask):
    return lax.ppermute(value, DEVICE_AXES, [(i, i ^ mask) for i in range(count)])


def all_sum(value, count):
    device_index = lax.axis_index(DEVICE_AXES)
    split = count > (1 << CORE_BIT)
    if split:
        core = (device_index >> CORE_BIT) & 1
        half = value.shape[0] // 2
        low, high = value[:half], value[half:]
        kept = jnp.where(core == 0, low, high)
        sent = jnp.where(core == 0, high, low)
        value = kept + exchange(sent, count, 1 << CORE_BIT)
    for group in exchange_stages(count):
        masks = []
        for size in range(1, len(group) + 1):
            for combo in itertools.combinations(group, size):
                masks.append(sum(1 << bit for bit in combo))
        received = [exchange(value, count, mask) for mask in masks]
        total = received[0]
        for part in received[1:]:
            total = total + part
        value = value + total
    if split:
        other = exchange(value, count, 1 << CORE_BIT)
        value = jnp.where(
            core == 0,
            jnp.concatenate([value, other], axis=0),
            jnp.concatenate([other, value], axis=0),
        )
    return value


def pack_gram(gram):
    half = gram.shape[0] // 2
    rows = lax.broadcasted_iota(jnp.int32, (half, half), 0)
    cols = lax.broadcasted_iota(jnp.int32, (half, half), 1)
    g11, g12, g22 = gram[:half, :half], gram[:half, half:], gram[half:, half:]
    tri = jnp.where(rows <= cols, g11, g22)
    diag = jnp.sum(jnp.where(rows == cols, g22, 0.0), axis=0, keepdims=True)
    extra = jnp.zeros((15, 2 * half), gram.dtype)
    extra_row = jnp.concatenate([diag, jnp.zeros_like(diag)], axis=1)
    return jnp.concatenate([jnp.concatenate([g12, tri], axis=1), extra_row, extra], axis=0)


def unpack_gram(packed, size):
    half = size // 2
    rows = lax.broadcasted_iota(jnp.int32, (half, half), 0)
    cols = lax.broadcasted_iota(jnp.int32, (half, half), 1)
    g12 = packed[:half, :half]
    tri = packed[:half, half:]
    diag = packed[half, :half]
    g11 = jnp.where(rows <= cols, tri, tri.T)
    g22 = jnp.where(rows > cols, tri, jnp.where(rows < cols, tri.T, jnp.diag(diag)))
    top = jnp.concatenate([g11, g12], axis=1)
    bottom = jnp.concatenate([g12.T, g22], axis=1)
    return jnp.concatenate([top, bottom], axis=0)


def cholesky_kernel(packed_ref, anomaly_ref, upper_ref, scores_ref, inverse_ref, work_ref, *, factor_scale, inverse_scale):
    size = packed_ref.shape[1]
    half = size // 2
    tri = packed_ref[:half, half:]
    g12 = packed_ref[:half, :half]
    diag = jnp.broadcast_to(packed_ref[half : half + 1, :half], (half, half))
    tri_t = jnp.transpose(tri)
    rows_h = lax.broadcasted_iota(jnp.int32, (half, half), 0)
    cols_h = lax.broadcasted_iota(jnp.int32, (half, half), 1)
    work_ref[:half, :half] = jnp.where(rows_h <= cols_h, tri, tri_t)
    work_ref[:half, half:] = g12
    work_ref[half:, :half] = jnp.transpose(g12)
    work_ref[half:, half:] = jnp.where(
        rows_h > cols_h, tri, jnp.where(rows_h < cols_h, tri_t, diag)
    )
    rows = lax.broadcasted_iota(jnp.int32, (size, size), 0)
    cols = lax.broadcasted_iota(jnp.int32, (size, size), 1)
    inverse_ref[...] = jnp.where(rows == cols, 1.0, 0.0).astype(jnp.float32)
    upper_ref[...] = jnp.zeros((size, size), jnp.float32)
    sub = lax.broadcasted_iota(jnp.int32, (PANEL, 1), 0)
    row_ids = lax.broadcasted_iota(jnp.int32, (size, 1), 0)
    def panel(first, row0, col0, col1):
        lane = lax.broadcasted_iota(jnp.int32, (1, size - col0), 1) + col0
        slab = work_ref[first:first + PANEL, col0:]
        inverse_slab = inverse_ref[first:first + PANEL, :col1]
        upper_slab = jnp.zeros((PANEL, size - col0), jnp.float32)
        for step in range(PANEL):
            column = first + step
            picked = slab[:, column - col0:column - col0 + 1]
            scale = lax.rsqrt(picked[step : step + 1, :])
            upper_row = jnp.where(lane >= column, slab[step : step + 1, :] * scale, 0.0)
            inverse_row = inverse_slab[step : step + 1, :] * scale
            coef = jnp.where(sub > step, picked * scale, 0.0)
            slab = slab - coef * upper_row
            inverse_slab = jnp.where(sub == step, inverse_row, inverse_slab - coef * inverse_row)
            upper_slab = jnp.where(sub == step, upper_row, upper_slab)
        upper_ref[first:first + PANEL, col0:] = upper_slab * factor_scale
        inverse_ref[first:first + PANEL, :col1] = inverse_slab * inverse_scale
        lower_cols = jnp.transpose(upper_slab)[row0 - col0:]
        lower_cols = jnp.where(row_ids[row0:] >= first + PANEL, lower_cols, 0.0)
        work_ref[row0:, col0:] = work_ref[row0:, col0:] - jnp.dot(
            lower_cols, upper_slab, precision=exact_mode, preferred_element_type=jnp.float32)
        inverse_ref[row0:, :col1] = inverse_ref[row0:, :col1] - jnp.dot(
            lower_cols, inverse_slab, precision=exact_mode, preferred_element_type=jnp.float32)

    quarter = size // 4
    for part in range(4):
        row0 = quarter * part
        col0 = (size // 2) * (part // 2)
        col1 = (size // 2) * (part // 2 + 1)
        for first in range(row0, row0 + quarter, PANEL):
            panel(first, row0, col0, col1)
    scores_ref[...] = lax.dot_general(
        anomaly_ref[...], inverse_ref[...], (((1,), (1,)), ((), ())),
        precision=exact_mode, preferred_element_type=jnp.float32,
    )


def cholesky_with_inverse(packed, anomaly, root):
    size = packed.shape[1]
    square = jax.ShapeDtypeStruct((size, size), jnp.float32)
    return pl.pallas_call(
        functools.partial(cholesky_kernel, factor_scale=1.0 / root, inverse_scale=root),
        out_shape=(square, jax.ShapeDtypeStruct(anomaly.shape, jnp.float32)),
        scratch_shapes=[pltpu.VMEM((size, size), jnp.float32), pltpu.VMEM((size, size), jnp.float32)],
    )(packed, anomaly)


def aggregate_kernel(zone_ref, base_ref, weight_ref, rows_ref, before_ref, own_ref, after_ref, work_ref):
    owned = own_ref.shape[0]
    work_ref[...] = jnp.zeros(work_ref.shape, work_ref.dtype)
    block_count, slot_count = weight_ref.shape[0], weight_ref.shape[1]
    for block in range(block_count):
        rows = rows_ref[block]
        for slot in range(slot_count):
            part = lax.dot_general(
                weight_ref[block, slot],
                rows,
                (((0,), (0,)), ((), ())),
                preferred_element_type=jnp.float32,
            )
            target = jnp.clip(zone_ref[slot, block] - base_ref[0], 0, 3 * owned - 1)
            work_ref[target] = work_ref[target] + part
    before_ref[...] = work_ref[:owned]
    own_ref[...] = work_ref[owned : 2 * owned]
    after_ref[...] = work_ref[2 * owned :]


def aggregate(zone_by_slot, base, weight_blocks, cell_rows, owned_blocks):
    block_size = weight_blocks.shape[3]
    day_count = cell_rows.shape[2]
    table = jax.ShapeDtypeStruct((owned_blocks, block_size, day_count), jnp.float32)
    return pl.pallas_call(
        aggregate_kernel,
        out_shape=(table, table, table),
        in_specs=[
            pl.BlockSpec(memory_space=pltpu.SMEM),
            pl.BlockSpec(memory_space=pltpu.SMEM),
            pl.BlockSpec(memory_space=pltpu.VMEM),
            pl.BlockSpec(memory_space=pltpu.VMEM),
        ],
        out_specs=(
            pl.BlockSpec(memory_space=pltpu.VMEM),
            pl.BlockSpec(memory_space=pltpu.VMEM),
            pl.BlockSpec(memory_space=pltpu.VMEM),
        ),
        scratch_shapes=[pltpu.VMEM((3 * owned_blocks, block_size, day_count), jnp.float32)],
    )(zone_by_slot, base, weight_blocks, cell_rows)


def body(runoff, weight_blocks, block_zone, climatology, zone_weight):
    block_count = weight_blocks.shape[0]
    block_size = weight_blocks.shape[2]
    day_count = runoff.shape[1]
    owned_blocks = climatology.shape[0] // block_size
    device_count = lax.axis_size(DEVICE_AXES)
    device_index = lax.axis_index(DEVICE_AXES)
    cell_rows = runoff.reshape(block_count, block_size, day_count)
    base = jnp.reshape((device_index - 1) * owned_blocks, (1,)).astype(jnp.int32)
    to_before, own_table, to_after = aggregate(
        block_zone.astype(jnp.int32).T, base, weight_blocks, cell_rows, owned_blocks
    )
    from_before = shifted(to_after, DEVICE_AXES, 1)
    from_after = shifted(to_before, DEVICE_AXES, -1)
    summed = own_table + from_before + from_after
    aggregated = summed.reshape(owned_blocks * block_size, day_count)
    anomaly = zone_weight[:, None] * (aggregated - climatology)
    local_gram = jnp.dot(
        anomaly.T, anomaly, precision=exact_mode, preferred_element_type=jnp.float32
    )
    local_gram = 0.5 * (local_gram + local_gram.T)
    total_packed = all_sum(pack_gram(local_gram), device_count)
    root = math.sqrt(anomaly.shape[0] * device_count)
    factor, scores = cholesky_with_inverse(total_packed, anomaly, root)
    return (scores, factor)


def solution(mesh):
    return jax.shard_map(
        body,
        mesh=mesh,
        in_specs=(
            P(DEVICE_AXES, None),
            P(DEVICE_AXES, None, None, None),
            P(DEVICE_AXES, None),
            P(DEVICE_AXES, None),
            P(DEVICE_AXES),
        ),
        out_specs=(P(DEVICE_AXES, None), P()),
        check_vma=False,
    )
```

```python
import functools
import itertools
import math

import jax
import jax.numpy as jnp
from jax import lax
from jax.experimental import pallas as pl
from jax.experimental.pallas import tpu as pltpu
from jax.sharding import PartitionSpec as P

exact_mode = lax.Precision.HIGHEST
DEVICE_AXES = ("lat", "sub")
CORE_BIT = 2
PANEL = 64


def shifted(value, axis, steps):
    count = lax.axis_size(axis)
    initial, last = (max(0, -steps), min(count, count - steps))
    return lax.ppermute(value, axis, [(source, source + steps) for source in range(initial, last)])


def exchange_stages(count):
    bits = count.bit_length() - 1
    groups, low = [], 0
    for width in (2, 1, 2, 2):
        if low >= bits:
            break
        if low != CORE_BIT:
            groups.append(list(range(low, min(bits, low + width))))
        low += width
    if low < bits:
        groups.append(list(range(low, bits)))
    return groups


def exchange(value, count, mask):
    return lax.ppermute(value, DEVICE_AXES, [(i, i ^ mask) for i in range(count)])


def all_sum(value, count):
    device_index = lax.axis_index(DEVICE_AXES)
    split = count > (1 << CORE_BIT)
    if split:
        core = (device_index >> CORE_BIT) & 1
        half = value.shape[0] // 2
        low, high = value[:half], value[half:]
        kept = jnp.where(core == 0, low, high)
        sent = jnp.where(core == 0, high, low)
        value = kept + exchange(sent, count, 1 << CORE_BIT)
    for group in reversed(exchange_stages(count)):
        masks = []
        for size in range(1, len(group) + 1):
            for combo in itertools.combinations(group, size):
                masks.append(sum(1 << bit for bit in combo))
        received = [exchange(value, count, mask) for mask in masks]
        total = received[0]
        for part in received[1:]:
            total = total + part
        value = value + total
    if split:
        other = exchange(value, count, 1 << CORE_BIT)
        value = jnp.where(
            core == 0,
            jnp.concatenate([value, other], axis=0),
            jnp.concatenate([other, value], axis=0),
        )
    return value


def pack_gram(gram):
    half = gram.shape[0] // 2
    rows = lax.broadcasted_iota(jnp.int32, (half, half), 0)
    cols = lax.broadcasted_iota(jnp.int32, (half, half), 1)
    g11, g12, g22 = gram[:half, :half], gram[:half, half:], gram[half:, half:]
    tri = jnp.where(rows <= cols, g11, g22)
    diag = jnp.sum(jnp.where(rows == cols, g22, 0.0), axis=0, keepdims=True)
    extra = jnp.zeros((15, 2 * half), gram.dtype)
    extra_row = jnp.concatenate([diag, jnp.zeros_like(diag)], axis=1)
    return jnp.concatenate([jnp.concatenate([g12, tri], axis=1), extra_row, extra], axis=0)


def unpack_gram(packed, size):
    half = size // 2
    rows = lax.broadcasted_iota(jnp.int32, (half, half), 0)
    cols = lax.broadcasted_iota(jnp.int32, (half, half), 1)
    g12 = packed[:half, :half]
    tri = packed[:half, half:]
    diag = packed[half, :half]
    g11 = jnp.where(rows <= cols, tri, tri.T)
    g22 = jnp.where(rows > cols, tri, jnp.where(rows < cols, tri.T, jnp.diag(diag)))
    top = jnp.concatenate([g11, g12], axis=1)
    bottom = jnp.concatenate([g12.T, g22], axis=1)
    return jnp.concatenate([top, bottom], axis=0)


def cholesky_kernel(packed_ref, anomaly_ref, upper_ref, scores_ref, inverse_ref, work_ref, *, factor_scale, inverse_scale):
    size = packed_ref.shape[1]
    half = size // 2
    tri = packed_ref[:half, half:]
    g12 = packed_ref[:half, :half]
    diag = jnp.broadcast_to(packed_ref[half : half + 1, :half], (half, half))
    tri_t = jnp.transpose(tri)
    rows_h = lax.broadcasted_iota(jnp.int32, (half, half), 0)
    cols_h = lax.broadcasted_iota(jnp.int32, (half, half), 1)
    work_ref[:half, :half] = jnp.where(rows_h <= cols_h, tri, tri_t)
    work_ref[:half, half:] = g12
    work_ref[half:, :half] = jnp.transpose(g12)
    work_ref[half:, half:] = jnp.where(
        rows_h > cols_h, tri, jnp.where(rows_h < cols_h, tri_t, diag)
    )
    rows = lax.broadcasted_iota(jnp.int32, (size, size), 0)
    cols = lax.broadcasted_iota(jnp.int32, (size, size), 1)
    inverse_ref[...] = jnp.where(rows == cols, 1.0, 0.0).astype(jnp.float32)
    upper_ref[...] = jnp.zeros((size, size), jnp.float32)
    sub = lax.broadcasted_iota(jnp.int32, (PANEL, 1), 0)
    row_ids = lax.broadcasted_iota(jnp.int32, (size, 1), 0)
    def panel(first, row0, col0, col1):
        lane = lax.broadcasted_iota(jnp.int32, (1, size - col0), 1) + col0
        slab = work_ref[first:first + PANEL, col0:]
        inverse_slab = inverse_ref[first:first + PANEL, :col1]
        upper_slab = jnp.zeros((PANEL, size - col0), jnp.float32)
        for step in range(PANEL):
            column = first + step
            picked = slab[:, column - col0:column - col0 + 1]
            scale = lax.rsqrt(picked[step : step + 1, :])
            upper_row = jnp.where(lane >= column, slab[step : step + 1, :] * scale, 0.0)
            inverse_row = inverse_slab[step : step + 1, :] * scale
            coef = jnp.where(sub > step, picked * scale, 0.0)
            slab = slab - coef * upper_row
            inverse_slab = jnp.where(sub == step, inverse_row, inverse_slab - coef * inverse_row)
            upper_slab = jnp.where(sub == step, upper_row, upper_slab)
        upper_ref[first:first + PANEL, col0:] = upper_slab * factor_scale
        inverse_ref[first:first + PANEL, :col1] = inverse_slab * inverse_scale
        lower_cols = jnp.transpose(upper_slab)[row0 - col0:]
        lower_cols = jnp.where(row_ids[row0:] >= first + PANEL, lower_cols, 0.0)
        work_ref[row0:, col0:] = work_ref[row0:, col0:] - jnp.dot(
            lower_cols, upper_slab, precision=exact_mode, preferred_element_type=jnp.float32)
        inverse_ref[row0:, :col1] = inverse_ref[row0:, :col1] - jnp.dot(
            lower_cols, inverse_slab, precision=exact_mode, preferred_element_type=jnp.float32)

    quarter = size // 4
    for part in range(4):
        row0 = quarter * part
        col0 = (size // 2) * (part // 2)
        col1 = (size // 2) * (part // 2 + 1)
        for first in range(row0, row0 + quarter, PANEL):
            panel(first, row0, col0, col1)
    scores_ref[...] = lax.dot_general(
        anomaly_ref[...], inverse_ref[...], (((1,), (1,)), ((), ())),
        precision=exact_mode, preferred_element_type=jnp.float32,
    )


def cholesky_with_inverse(packed, anomaly, root):
    size = packed.shape[1]
    square = jax.ShapeDtypeStruct((size, size), jnp.float32)
    return pl.pallas_call(
        functools.partial(cholesky_kernel, factor_scale=1.0 / root, inverse_scale=root),
        out_shape=(square, jax.ShapeDtypeStruct(anomaly.shape, jnp.float32)),
        scratch_shapes=[pltpu.VMEM((size, size), jnp.float32), pltpu.VMEM((size, size), jnp.float32)],
    )(packed, anomaly)


def aggregate_kernel(zone_ref, base_ref, weight_ref, rows_ref, before_ref, own_ref, after_ref, work_ref):
    owned = own_ref.shape[0]
    work_ref[...] = jnp.zeros(work_ref.shape, work_ref.dtype)
    block_count, slot_count = weight_ref.shape[0], weight_ref.shape[1]
    for block in range(block_count):
        rows = rows_ref[block]
        for slot in range(slot_count):
            part = lax.dot_general(
                weight_ref[block, slot],
                rows,
                (((0,), (0,)), ((), ())),
                preferred_element_type=jnp.float32,
            )
            target = jnp.clip(zone_ref[slot, block] - base_ref[0], 0, 3 * owned - 1)
            work_ref[target] = work_ref[target] + part
    before_ref[...] = work_ref[:owned]
    own_ref[...] = work_ref[owned : 2 * owned]
    after_ref[...] = work_ref[2 * owned :]


def aggregate(zone_by_slot, base, weight_blocks, cell_rows, owned_blocks):
    block_size = weight_blocks.shape[3]
    day_count = cell_rows.shape[2]
    table = jax.ShapeDtypeStruct((owned_blocks, block_size, day_count), jnp.float32)
    return pl.pallas_call(
        aggregate_kernel,
        out_shape=(table, table, table),
        in_specs=[
            pl.BlockSpec(memory_space=pltpu.SMEM),
            pl.BlockSpec(memory_space=pltpu.SMEM),
            pl.BlockSpec(memory_space=pltpu.VMEM),
            pl.BlockSpec(memory_space=pltpu.VMEM),
        ],
        out_specs=(
            pl.BlockSpec(memory_space=pltpu.VMEM),
            pl.BlockSpec(memory_space=pltpu.VMEM),
            pl.BlockSpec(memory_space=pltpu.VMEM),
        ),
        scratch_shapes=[pltpu.VMEM((3 * owned_blocks, block_size, day_count), jnp.float32)],
    )(zone_by_slot, base, weight_blocks, cell_rows)


def body(runoff, weight_blocks, block_zone, climatology, zone_weight):
    block_count = weight_blocks.shape[0]
    block_size = weight_blocks.shape[2]
    day_count = runoff.shape[1]
    owned_blocks = climatology.shape[0] // block_size
    device_count = lax.axis_size(DEVICE_AXES)
    device_index = lax.axis_index(DEVICE_AXES)
    cell_rows = runoff.reshape(block_count, block_size, day_count)
    base = jnp.reshape((device_index - 1) * owned_blocks, (1,)).astype(jnp.int32)
    to_before, own_table, to_after = aggregate(
        block_zone.astype(jnp.int32).T, base, weight_blocks, cell_rows, owned_blocks
    )
    from_before = shifted(to_after, DEVICE_AXES, 1)
    from_after = shifted(to_before, DEVICE_AXES, -1)
    summed = own_table + from_before + from_after
    aggregated = summed.reshape(owned_blocks * block_size, day_count)
    anomaly = zone_weight[:, None] * (aggregated - climatology)
    local_gram = jnp.dot(
        anomaly.T, anomaly, precision=exact_mode, preferred_element_type=jnp.float32
    )
    local_gram = 0.5 * (local_gram + local_gram.T)
    total_packed = all_sum(pack_gram(local_gram), device_count)
    root = math.sqrt(anomaly.shape[0] * device_count)
    factor, scores = cholesky_with_inverse(total_packed, anomaly, root)
    return (scores, factor)


def solution(mesh):
    return jax.shard_map(
        body,
        mesh=mesh,
        in_specs=(
            P(DEVICE_AXES, None),
            P(DEVICE_AXES, None, None, None),
            P(DEVICE_AXES, None),
            P(DEVICE_AXES, None),
            P(DEVICE_AXES),
        ),
        out_specs=(P(DEVICE_AXES, None), P()),
        check_vma=False,
    )
```

```python
import functools
import itertools
import math

import jax
import jax.numpy as jnp
from jax import lax
from jax.experimental import pallas as pl
from jax.experimental.pallas import tpu as pltpu
from jax.sharding import PartitionSpec as P

exact_mode = lax.Precision.HIGHEST
DEVICE_AXES = ("lat", "sub")
CORE_BIT = 2
PANEL = 32


def shifted(value, axis, steps):
    count = lax.axis_size(axis)
    initial, last = (max(0, -steps), min(count, count - steps))
    return lax.ppermute(value, axis, [(source, source + steps) for source in range(initial, last)])


def exchange_stages(count):
    bits = count.bit_length() - 1
    groups, low = [], 0
    for width in (2, 1, 2, 2):
        if low >= bits:
            break
        if low != CORE_BIT:
            groups.append(list(range(low, min(bits, low + width))))
        low += width
    if low < bits:
        groups.append(list(range(low, bits)))
    return groups


def exchange(value, count, mask):
    return lax.ppermute(value, DEVICE_AXES, [(i, i ^ mask) for i in range(count)])


def all_sum(value, count):
    device_index = lax.axis_index(DEVICE_AXES)
    split = count > (1 << CORE_BIT)
    if split:
        core = (device_index >> CORE_BIT) & 1
        half = value.shape[0] // 2
        low, high = value[:half], value[half:]
        kept = jnp.where(core == 0, low, high)
        sent = jnp.where(core == 0, high, low)
        value = kept + exchange(sent, count, 1 << CORE_BIT)
    for group in exchange_stages(count):
        masks = []
        for size in range(1, len(group) + 1):
            for combo in itertools.combinations(group, size):
                masks.append(sum(1 << bit for bit in combo))
        received = [exchange(value, count, mask) for mask in masks]
        total = received[0]
        for part in received[1:]:
            total = total + part
        value = value + total
    if split:
        other = exchange(value, count, 1 << CORE_BIT)
        value = jnp.where(
            core == 0,
            jnp.concatenate([value, other], axis=0),
            jnp.concatenate([other, value], axis=0),
        )
    return value


def pack_gram(gram):
    half = gram.shape[0] // 2
    rows = lax.broadcasted_iota(jnp.int32, (half, half), 0)
    cols = lax.broadcasted_iota(jnp.int32, (half, half), 1)
    g11, g12, g22 = gram[:half, :half], gram[:half, half:], gram[half:, half:]
    tri = jnp.where(rows <= cols, g11, g22)
    diag = jnp.sum(jnp.where(rows == cols, g22, 0.0), axis=0, keepdims=True)
    extra = jnp.zeros((15, 2 * half), gram.dtype)
    extra_row = jnp.concatenate([diag, jnp.zeros_like(diag)], axis=1)
    return jnp.concatenate([jnp.concatenate([g12, tri], axis=1), extra_row, extra], axis=0)


def unpack_gram(packed, size):
    half = size // 2
    rows = lax.broadcasted_iota(jnp.int32, (half, half), 0)
    cols = lax.broadcasted_iota(jnp.int32, (half, half), 1)
    g12 = packed[:half, :half]
    tri = packed[:half, half:]
    diag = packed[half, :half]
    g11 = jnp.where(rows <= cols, tri, tri.T)
    g22 = jnp.where(rows > cols, tri, jnp.where(rows < cols, tri.T, jnp.diag(diag)))
    top = jnp.concatenate([g11, g12], axis=1)
    bottom = jnp.concatenate([g12.T, g22], axis=1)
    return jnp.concatenate([top, bottom], axis=0)


def cholesky_kernel(packed_ref, anomaly_ref, upper_ref, scores_ref, inverse_ref, work_ref, *, factor_scale, inverse_scale):
    size = packed_ref.shape[1]
    half = size // 2
    tri = packed_ref[:half, half:]
    g12 = packed_ref[:half, :half]
    diag = jnp.broadcast_to(packed_ref[half : half + 1, :half], (half, half))
    tri_t = jnp.transpose(tri)
    rows_h = lax.broadcasted_iota(jnp.int32, (half, half), 0)
    cols_h = lax.broadcasted_iota(jnp.int32, (half, half), 1)
    work_ref[:half, :half] = jnp.where(rows_h <= cols_h, tri, tri_t)
    work_ref[:half, half:] = g12
    work_ref[half:, :half] = jnp.transpose(g12)
    work_ref[half:, half:] = jnp.where(
        rows_h > cols_h, tri, jnp.where(rows_h < cols_h, tri_t, diag)
    )
    rows = lax.broadcasted_iota(jnp.int32, (size, size), 0)
    cols = lax.broadcasted_iota(jnp.int32, (size, size), 1)
    inverse_ref[...] = jnp.where(rows == cols, 1.0, 0.0).astype(jnp.float32)
    upper_ref[...] = jnp.zeros((size, size), jnp.float32)
    sub = lax.broadcasted_iota(jnp.int32, (PANEL, 1), 0)
    row_ids = lax.broadcasted_iota(jnp.int32, (size, 1), 0)
    def panel(first, row0, col0, col1):
        lane = lax.broadcasted_iota(jnp.int32, (1, size - col0), 1) + col0
        slab = work_ref[first:first + PANEL, col0:]
        inverse_slab = inverse_ref[first:first + PANEL, :col1]
        upper_slab = jnp.zeros((PANEL, size - col0), jnp.float32)
        for step in range(PANEL):
            column = first + step
            picked = slab[:, column - col0:column - col0 + 1]
            scale = lax.rsqrt(picked[step : step + 1, :])
            upper_row = jnp.where(lane >= column, slab[step : step + 1, :] * scale, 0.0)
            inverse_row = inverse_slab[step : step + 1, :] * scale
            coef = jnp.where(sub > step, picked * scale, 0.0)
            slab = slab - coef * upper_row
            inverse_slab = jnp.where(sub == step, inverse_row, inverse_slab - coef * inverse_row)
            upper_slab = jnp.where(sub == step, upper_row, upper_slab)
        upper_ref[first:first + PANEL, col0:] = upper_slab * factor_scale
        inverse_ref[first:first + PANEL, :col1] = inverse_slab * inverse_scale
        lower_cols = jnp.transpose(upper_slab)[row0 - col0:]
        lower_cols = jnp.where(row_ids[row0:] >= first + PANEL, lower_cols, 0.0)
        work_ref[row0:, col0:] = work_ref[row0:, col0:] - jnp.dot(
            lower_cols, upper_slab, precision=exact_mode, preferred_element_type=jnp.float32)
        inverse_ref[row0:, :col1] = inverse_ref[row0:, :col1] - jnp.dot(
            lower_cols, inverse_slab, precision=exact_mode, preferred_element_type=jnp.float32)

    quarter = size // 4
    for part in range(4):
        row0 = quarter * part
        col0 = (size // 2) * (part // 2)
        col1 = (size // 2) * (part // 2 + 1)
        for first in range(row0, row0 + quarter, PANEL):
            panel(first, row0, col0, col1)
    scores_ref[...] = lax.dot_general(
        anomaly_ref[...], inverse_ref[...], (((1,), (1,)), ((), ())),
        precision=exact_mode, preferred_element_type=jnp.float32,
    )


def cholesky_with_inverse(packed, anomaly, root):
    size = packed.shape[1]
    square = jax.ShapeDtypeStruct((size, size), jnp.float32)
    return pl.pallas_call(
        functools.partial(cholesky_kernel, factor_scale=1.0 / root, inverse_scale=root),
        out_shape=(square, jax.ShapeDtypeStruct(anomaly.shape, jnp.float32)),
        scratch_shapes=[pltpu.VMEM((size, size), jnp.float32), pltpu.VMEM((size, size), jnp.float32)],
    )(packed, anomaly)


def aggregate_kernel(zone_ref, base_ref, weight_ref, rows_ref, before_ref, own_ref, after_ref, work_ref):
    owned = own_ref.shape[0]
    work_ref[...] = jnp.zeros(work_ref.shape, work_ref.dtype)
    block_count, slot_count = weight_ref.shape[0], weight_ref.shape[1]
    for block in range(block_count):
        rows = rows_ref[block]
        for slot in range(slot_count):
            part = lax.dot_general(
                weight_ref[block, slot],
                rows,
                (((0,), (0,)), ((), ())),
                preferred_element_type=jnp.float32,
            )
            target = jnp.clip(zone_ref[slot, block] - base_ref[0], 0, 3 * owned - 1)
            work_ref[target] = work_ref[target] + part
    before_ref[...] = work_ref[:owned]
    own_ref[...] = work_ref[owned : 2 * owned]
    after_ref[...] = work_ref[2 * owned :]


def aggregate(zone_by_slot, base, weight_blocks, cell_rows, owned_blocks):
    block_size = weight_blocks.shape[3]
    day_count = cell_rows.shape[2]
    table = jax.ShapeDtypeStruct((owned_blocks, block_size, day_count), jnp.float32)
    return pl.pallas_call(
        aggregate_kernel,
        out_shape=(table, table, table),
        in_specs=[
            pl.BlockSpec(memory_space=pltpu.SMEM),
            pl.BlockSpec(memory_space=pltpu.SMEM),
            pl.BlockSpec(memory_space=pltpu.VMEM),
            pl.BlockSpec(memory_space=pltpu.VMEM),
        ],
        out_specs=(
            pl.BlockSpec(memory_space=pltpu.VMEM),
            pl.BlockSpec(memory_space=pltpu.VMEM),
            pl.BlockSpec(memory_space=pltpu.VMEM),
        ),
        scratch_shapes=[pltpu.VMEM((3 * owned_blocks, block_size, day_count), jnp.float32)],
    )(zone_by_slot, base, weight_blocks, cell_rows)


def body(runoff, weight_blocks, block_zone, climatology, zone_weight):
    block_count = weight_blocks.shape[0]
    block_size = weight_blocks.shape[2]
    day_count = runoff.shape[1]
    owned_blocks = climatology.shape[0] // block_size
    device_count = lax.axis_size(DEVICE_AXES)
    device_index = lax.axis_index(DEVICE_AXES)
    cell_rows = runoff.reshape(block_count, block_size, day_count)
    base = jnp.reshape((device_index - 1) * owned_blocks, (1,)).astype(jnp.int32)
    to_before, own_table, to_after = aggregate(
        block_zone.astype(jnp.int32).T, base, weight_blocks, cell_rows, owned_blocks
    )
    from_before = shifted(to_after, DEVICE_AXES, 1)
    from_after = shifted(to_before, DEVICE_AXES, -1)
    summed = own_table + from_before + from_after
    aggregated = summed.reshape(owned_blocks * block_size, day_count)
    anomaly = zone_weight[:, None] * (aggregated - climatology)
    local_gram = jnp.dot(
        anomaly.T, anomaly, precision=exact_mode, preferred_element_type=jnp.float32
    )
    local_gram = 0.5 * (local_gram + local_gram.T)
    total_packed = all_sum(pack_gram(local_gram), device_count)
    root = math.sqrt(anomaly.shape[0] * device_count)
    factor, scores = cholesky_with_inverse(total_packed, anomaly, root)
    return (scores, factor)


def solution(mesh):
    return jax.shard_map(
        body,
        mesh=mesh,
        in_specs=(
            P(DEVICE_AXES, None),
            P(DEVICE_AXES, None, None, None),
            P(DEVICE_AXES, None),
            P(DEVICE_AXES, None),
            P(DEVICE_AXES),
        ),
        out_specs=(P(DEVICE_AXES, None), P()),
        check_vma=False,
    )
```

```python
import functools
import itertools
import math

import jax
import jax.numpy as jnp
from jax import lax
from jax.experimental import pallas as pl
from jax.experimental.pallas import tpu as pltpu
from jax.sharding import PartitionSpec as P

exact_mode = lax.Precision.HIGHEST
DEVICE_AXES = ("lat", "sub")
CORE_BIT = 2
PANEL = 128


def shifted(value, axis, steps):
    count = lax.axis_size(axis)
    initial, last = (max(0, -steps), min(count, count - steps))
    return lax.ppermute(value, axis, [(source, source + steps) for source in range(initial, last)])


def exchange_stages(count):
    bits = count.bit_length() - 1
    groups, low = [], 0
    for width in (2, 1, 2, 2):
        if low >= bits:
            break
        if low != CORE_BIT:
            groups.append(list(range(low, min(bits, low + width))))
        low += width
    if low < bits:
        groups.append(list(range(low, bits)))
    return groups


def exchange(value, count, mask):
    return lax.ppermute(value, DEVICE_AXES, [(i, i ^ mask) for i in range(count)])


def all_sum(value, count):
    device_index = lax.axis_index(DEVICE_AXES)
    split = count > (1 << CORE_BIT)
    if split:
        core = (device_index >> CORE_BIT) & 1
        half = value.shape[0] // 2
        low, high = value[:half], value[half:]
        kept = jnp.where(core == 0, low, high)
        sent = jnp.where(core == 0, high, low)
        value = kept + exchange(sent, count, 1 << CORE_BIT)
    for group in exchange_stages(count):
        masks = []
        for size in range(1, len(group) + 1):
            for combo in itertools.combinations(group, size):
                masks.append(sum(1 << bit for bit in combo))
        received = [exchange(value, count, mask) for mask in masks]
        total = received[0]
        for part in received[1:]:
            total = total + part
        value = value + total
    if split:
        other = exchange(value, count, 1 << CORE_BIT)
        value = jnp.where(
            core == 0,
            jnp.concatenate([value, other], axis=0),
            jnp.concatenate([other, value], axis=0),
        )
    return value


def pack_gram(gram):
    half = gram.shape[0] // 2
    rows = lax.broadcasted_iota(jnp.int32, (half, half), 0)
    cols = lax.broadcasted_iota(jnp.int32, (half, half), 1)
    g11, g12, g22 = gram[:half, :half], gram[:half, half:], gram[half:, half:]
    tri = jnp.where(rows <= cols, g11, g22)
    diag = jnp.sum(jnp.where(rows == cols, g22, 0.0), axis=0, keepdims=True)
    extra = jnp.zeros((15, 2 * half), gram.dtype)
    extra_row = jnp.concatenate([diag, jnp.zeros_like(diag)], axis=1)
    return jnp.concatenate([jnp.concatenate([g12, tri], axis=1), extra_row, extra], axis=0)


def unpack_gram(packed, size):
    half = size // 2
    rows = lax.broadcasted_iota(jnp.int32, (half, half), 0)
    cols = lax.broadcasted_iota(jnp.int32, (half, half), 1)
    g12 = packed[:half, :half]
    tri = packed[:half, half:]
    diag = packed[half, :half]
    g11 = jnp.where(rows <= cols, tri, tri.T)
    g22 = jnp.where(rows > cols, tri, jnp.where(rows < cols, tri.T, jnp.diag(diag)))
    top = jnp.concatenate([g11, g12], axis=1)
    bottom = jnp.concatenate([g12.T, g22], axis=1)
    return jnp.concatenate([top, bottom], axis=0)


def cholesky_kernel(packed_ref, anomaly_ref, upper_ref, scores_ref, inverse_ref, work_ref, *, factor_scale, inverse_scale):
    size = packed_ref.shape[1]
    half = size // 2
    tri = packed_ref[:half, half:]
    g12 = packed_ref[:half, :half]
    diag = jnp.broadcast_to(packed_ref[half : half + 1, :half], (half, half))
    tri_t = jnp.transpose(tri)
    rows_h = lax.broadcasted_iota(jnp.int32, (half, half), 0)
    cols_h = lax.broadcasted_iota(jnp.int32, (half, half), 1)
    work_ref[:half, :half] = jnp.where(rows_h <= cols_h, tri, tri_t)
    work_ref[:half, half:] = g12
    work_ref[half:, :half] = jnp.transpose(g12)
    work_ref[half:, half:] = jnp.where(
        rows_h > cols_h, tri, jnp.where(rows_h < cols_h, tri_t, diag)
    )
    rows = lax.broadcasted_iota(jnp.int32, (size, size), 0)
    cols = lax.broadcasted_iota(jnp.int32, (size, size), 1)
    inverse_ref[...] = jnp.where(rows == cols, 1.0, 0.0).astype(jnp.float32)
    upper_ref[...] = jnp.zeros((size, size), jnp.float32)
    sub = lax.broadcasted_iota(jnp.int32, (PANEL, 1), 0)
    row_ids = lax.broadcasted_iota(jnp.int32, (size, 1), 0)
    def panel(first, row0, col0, col1):
        lane = lax.broadcasted_iota(jnp.int32, (1, size - col0), 1) + col0
        slab = work_ref[first:first + PANEL, col0:]
        inverse_slab = inverse_ref[first:first + PANEL, :col1]
        upper_slab = jnp.zeros((PANEL, size - col0), jnp.float32)
        for step in range(PANEL):
            column = first + step
            picked = slab[:, column - col0:column - col0 + 1]
            scale = lax.rsqrt(picked[step : step + 1, :])
            upper_row = jnp.where(lane >= column, slab[step : step + 1, :] * scale, 0.0)
            inverse_row = inverse_slab[step : step + 1, :] * scale
            coef = jnp.where(sub > step, picked * scale, 0.0)
            slab = slab - coef * upper_row
            inverse_slab = jnp.where(sub == step, inverse_row, inverse_slab - coef * inverse_row)
            upper_slab = jnp.where(sub == step, upper_row, upper_slab)
        upper_ref[first:first + PANEL, col0:] = upper_slab * factor_scale
        inverse_ref[first:first + PANEL, :col1] = inverse_slab * inverse_scale
        lower_cols = jnp.transpose(upper_slab)[row0 - col0:]
        lower_cols = jnp.where(row_ids[row0:] >= first + PANEL, lower_cols, 0.0)
        work_ref[row0:, col0:] = work_ref[row0:, col0:] - jnp.dot(
            lower_cols, upper_slab, precision=exact_mode, preferred_element_type=jnp.float32)
        inverse_ref[row0:, :col1] = inverse_ref[row0:, :col1] - jnp.dot(
            lower_cols, inverse_slab, precision=exact_mode, preferred_element_type=jnp.float32)

    part_rows = max(PANEL, size // 4)
    for row0 in range(0, size, part_rows):
        col0 = (size // 2) * (row0 // (size // 2))
        col1 = col0 + size // 2
        for first in range(row0, row0 + part_rows, PANEL):
            panel(first, row0, col0, col1)
    scores_ref[...] = lax.dot_general(
        anomaly_ref[...], inverse_ref[...], (((1,), (1,)), ((), ())),
        precision=exact_mode, preferred_element_type=jnp.float32,
    )


def cholesky_with_inverse(packed, anomaly, root):
    size = packed.shape[1]
    square = jax.ShapeDtypeStruct((size, size), jnp.float32)
    return pl.pallas_call(
        functools.partial(cholesky_kernel, factor_scale=1.0 / root, inverse_scale=root),
        out_shape=(square, jax.ShapeDtypeStruct(anomaly.shape, jnp.float32)),
        scratch_shapes=[pltpu.VMEM((size, size), jnp.float32), pltpu.VMEM((size, size), jnp.float32)],
    )(packed, anomaly)


def aggregate_kernel(zone_ref, base_ref, weight_ref, rows_ref, before_ref, own_ref, after_ref, work_ref):
    owned = own_ref.shape[0]
    work_ref[...] = jnp.zeros(work_ref.shape, work_ref.dtype)
    block_count, slot_count = weight_ref.shape[0], weight_ref.shape[1]
    for block in range(block_count):
        rows = rows_ref[block]
        for slot in range(slot_count):
            part = lax.dot_general(
                weight_ref[block, slot],
                rows,
                (((0,), (0,)), ((), ())),
                preferred_element_type=jnp.float32,
            )
            target = jnp.clip(zone_ref[slot, block] - base_ref[0], 0, 3 * owned - 1)
            work_ref[target] = work_ref[target] + part
    before_ref[...] = work_ref[:owned]
    own_ref[...] = work_ref[owned : 2 * owned]
    after_ref[...] = work_ref[2 * owned :]


def aggregate(zone_by_slot, base, weight_blocks, cell_rows, owned_blocks):
    block_size = weight_blocks.shape[3]
    day_count = cell_rows.shape[2]
    table = jax.ShapeDtypeStruct((owned_blocks, block_size, day_count), jnp.float32)
    return pl.pallas_call(
        aggregate_kernel,
        out_shape=(table, table, table),
        in_specs=[
            pl.BlockSpec(memory_space=pltpu.SMEM),
            pl.BlockSpec(memory_space=pltpu.SMEM),
            pl.BlockSpec(memory_space=pltpu.VMEM),
            pl.BlockSpec(memory_space=pltpu.VMEM),
        ],
        out_specs=(
            pl.BlockSpec(memory_space=pltpu.VMEM),
            pl.BlockSpec(memory_space=pltpu.VMEM),
            pl.BlockSpec(memory_space=pltpu.VMEM),
        ),
        scratch_shapes=[pltpu.VMEM((3 * owned_blocks, block_size, day_count), jnp.float32)],
    )(zone_by_slot, base, weight_blocks, cell_rows)


def body(runoff, weight_blocks, block_zone, climatology, zone_weight):
    block_count = weight_blocks.shape[0]
    block_size = weight_blocks.shape[2]
    day_count = runoff.shape[1]
    owned_blocks = climatology.shape[0] // block_size
    device_count = lax.axis_size(DEVICE_AXES)
    device_index = lax.axis_index(DEVICE_AXES)
    cell_rows = runoff.reshape(block_count, block_size, day_count)
    base = jnp.reshape((device_index - 1) * owned_blocks, (1,)).astype(jnp.int32)
    to_before, own_table, to_after = aggregate(
        block_zone.astype(jnp.int32).T, base, weight_blocks, cell_rows, owned_blocks
    )
    from_before = shifted(to_after, DEVICE_AXES, 1)
    from_after = shifted(to_before, DEVICE_AXES, -1)
    summed = own_table + from_before + from_after
    aggregated = summed.reshape(owned_blocks * block_size, day_count)
    anomaly = zone_weight[:, None] * (aggregated - climatology)
    local_gram = jnp.dot(
        anomaly.T, anomaly, precision=exact_mode, preferred_element_type=jnp.float32
    )
    local_gram = 0.5 * (local_gram + local_gram.T)
    total_packed = all_sum(pack_gram(local_gram), device_count)
    root = math.sqrt(anomaly.shape[0] * device_count)
    factor, scores = cholesky_with_inverse(total_packed, anomaly, root)
    return (scores, factor)


def solution(mesh):
    return jax.shard_map(
        body,
        mesh=mesh,
        in_specs=(
            P(DEVICE_AXES, None),
            P(DEVICE_AXES, None, None, None),
            P(DEVICE_AXES, None),
            P(DEVICE_AXES, None),
            P(DEVICE_AXES),
        ),
        out_specs=(P(DEVICE_AXES, None), P()),
        check_vma=False,
    )
```

```python
import functools
import itertools
import math

import jax
import jax.numpy as jnp
from jax import lax
from jax.experimental import pallas as pl
from jax.experimental.pallas import tpu as pltpu
from jax.sharding import PartitionSpec as P

exact_mode = lax.Precision.HIGHEST
DEVICE_AXES = ("lat", "sub")
CORE_BIT = 2
PANEL = 256


def shifted(value, axis, steps):
    count = lax.axis_size(axis)
    initial, last = (max(0, -steps), min(count, count - steps))
    return lax.ppermute(value, axis, [(source, source + steps) for source in range(initial, last)])


def exchange_stages(count):
    bits = count.bit_length() - 1
    groups, low = [], 0
    for width in (2, 1, 2, 2):
        if low >= bits:
            break
        if low != CORE_BIT:
            groups.append(list(range(low, min(bits, low + width))))
        low += width
    if low < bits:
        groups.append(list(range(low, bits)))
    return groups


def exchange(value, count, mask):
    return lax.ppermute(value, DEVICE_AXES, [(i, i ^ mask) for i in range(count)])


def all_sum(value, count):
    device_index = lax.axis_index(DEVICE_AXES)
    split = count > (1 << CORE_BIT)
    if split:
        core = (device_index >> CORE_BIT) & 1
        half = value.shape[0] // 2
        low, high = value[:half], value[half:]
        kept = jnp.where(core == 0, low, high)
        sent = jnp.where(core == 0, high, low)
        value = kept + exchange(sent, count, 1 << CORE_BIT)
    for group in exchange_stages(count):
        masks = []
        for size in range(1, len(group) + 1):
            for combo in itertools.combinations(group, size):
                masks.append(sum(1 << bit for bit in combo))
        received = [exchange(value, count, mask) for mask in masks]
        total = received[0]
        for part in received[1:]:
            total = total + part
        value = value + total
    if split:
        other = exchange(value, count, 1 << CORE_BIT)
        value = jnp.where(
            core == 0,
            jnp.concatenate([value, other], axis=0),
            jnp.concatenate([other, value], axis=0),
        )
    return value


def pack_gram(gram):
    half = gram.shape[0] // 2
    rows = lax.broadcasted_iota(jnp.int32, (half, half), 0)
    cols = lax.broadcasted_iota(jnp.int32, (half, half), 1)
    g11, g12, g22 = gram[:half, :half], gram[:half, half:], gram[half:, half:]
    tri = jnp.where(rows <= cols, g11, g22)
    diag = jnp.sum(jnp.where(rows == cols, g22, 0.0), axis=0, keepdims=True)
    extra = jnp.zeros((15, 2 * half), gram.dtype)
    extra_row = jnp.concatenate([diag, jnp.zeros_like(diag)], axis=1)
    return jnp.concatenate([jnp.concatenate([g12, tri], axis=1), extra_row, extra], axis=0)


def unpack_gram(packed, size):
    half = size // 2
    rows = lax.broadcasted_iota(jnp.int32, (half, half), 0)
    cols = lax.broadcasted_iota(jnp.int32, (half, half), 1)
    g12 = packed[:half, :half]
    tri = packed[:half, half:]
    diag = packed[half, :half]
    g11 = jnp.where(rows <= cols, tri, tri.T)
    g22 = jnp.where(rows > cols, tri, jnp.where(rows < cols, tri.T, jnp.diag(diag)))
    top = jnp.concatenate([g11, g12], axis=1)
    bottom = jnp.concatenate([g12.T, g22], axis=1)
    return jnp.concatenate([top, bottom], axis=0)


def cholesky_kernel(packed_ref, anomaly_ref, upper_ref, scores_ref, inverse_ref, work_ref, *, factor_scale, inverse_scale):
    size = packed_ref.shape[1]
    half = size // 2
    tri = packed_ref[:half, half:]
    g12 = packed_ref[:half, :half]
    diag = jnp.broadcast_to(packed_ref[half : half + 1, :half], (half, half))
    tri_t = jnp.transpose(tri)
    rows_h = lax.broadcasted_iota(jnp.int32, (half, half), 0)
    cols_h = lax.broadcasted_iota(jnp.int32, (half, half), 1)
    work_ref[:half, :half] = jnp.where(rows_h <= cols_h, tri, tri_t)
    work_ref[:half, half:] = g12
    work_ref[half:, :half] = jnp.transpose(g12)
    work_ref[half:, half:] = jnp.where(
        rows_h > cols_h, tri, jnp.where(rows_h < cols_h, tri_t, diag)
    )
    rows = lax.broadcasted_iota(jnp.int32, (size, size), 0)
    cols = lax.broadcasted_iota(jnp.int32, (size, size), 1)
    inverse_ref[...] = jnp.where(rows == cols, 1.0, 0.0).astype(jnp.float32)
    upper_ref[...] = jnp.zeros((size, size), jnp.float32)
    sub = lax.broadcasted_iota(jnp.int32, (PANEL, 1), 0)
    row_ids = lax.broadcasted_iota(jnp.int32, (size, 1), 0)
    def panel(first, row0, col0, col1):
        lane = lax.broadcasted_iota(jnp.int32, (1, size - col0), 1) + col0
        slab = work_ref[first:first + PANEL, col0:]
        inverse_slab = inverse_ref[first:first + PANEL, :col1]
        upper_slab = jnp.zeros((PANEL, size - col0), jnp.float32)
        for step in range(PANEL):
            column = first + step
            picked = slab[:, column - col0:column - col0 + 1]
            scale = lax.rsqrt(picked[step : step + 1, :])
            upper_row = jnp.where(lane >= column, slab[step : step + 1, :] * scale, 0.0)
            inverse_row = inverse_slab[step : step + 1, :] * scale
            coef = jnp.where(sub > step, picked * scale, 0.0)
            slab = slab - coef * upper_row
            inverse_slab = jnp.where(sub == step, inverse_row, inverse_slab - coef * inverse_row)
            upper_slab = jnp.where(sub == step, upper_row, upper_slab)
        upper_ref[first:first + PANEL, col0:] = upper_slab * factor_scale
        inverse_ref[first:first + PANEL, :col1] = inverse_slab * inverse_scale
        lower_cols = jnp.transpose(upper_slab)[row0 - col0:]
        lower_cols = jnp.where(row_ids[row0:] >= first + PANEL, lower_cols, 0.0)
        work_ref[row0:, col0:] = work_ref[row0:, col0:] - jnp.dot(
            lower_cols, upper_slab, precision=exact_mode, preferred_element_type=jnp.float32)
        inverse_ref[row0:, :col1] = inverse_ref[row0:, :col1] - jnp.dot(
            lower_cols, inverse_slab, precision=exact_mode, preferred_element_type=jnp.float32)

    part_rows = max(PANEL, size // 4)
    for row0 in range(0, size, part_rows):
        col0 = (size // 2) * (row0 // (size // 2))
        col1 = -(-(row0 + part_rows) // (size // 2)) * (size // 2)
        for first in range(row0, row0 + part_rows, PANEL):
            panel(first, row0, col0, col1)
    scores_ref[...] = lax.dot_general(
        anomaly_ref[...], inverse_ref[...], (((1,), (1,)), ((), ())),
        precision=exact_mode, preferred_element_type=jnp.float32,
    )


def cholesky_with_inverse(packed, anomaly, root):
    size = packed.shape[1]
    square = jax.ShapeDtypeStruct((size, size), jnp.float32)
    return pl.pallas_call(
        functools.partial(cholesky_kernel, factor_scale=1.0 / root, inverse_scale=root),
        out_shape=(square, jax.ShapeDtypeStruct(anomaly.shape, jnp.float32)),
        scratch_shapes=[pltpu.VMEM((size, size), jnp.float32), pltpu.VMEM((size, size), jnp.float32)],
    )(packed, anomaly)


def aggregate_kernel(zone_ref, base_ref, weight_ref, rows_ref, before_ref, own_ref, after_ref, work_ref):
    owned = own_ref.shape[0]
    work_ref[...] = jnp.zeros(work_ref.shape, work_ref.dtype)
    block_count, slot_count = weight_ref.shape[0], weight_ref.shape[1]
    for block in range(block_count):
        rows = rows_ref[block]
        for slot in range(slot_count):
            part = lax.dot_general(
                weight_ref[block, slot],
                rows,
                (((0,), (0,)), ((), ())),
                preferred_element_type=jnp.float32,
            )
            target = jnp.clip(zone_ref[slot, block] - base_ref[0], 0, 3 * owned - 1)
            work_ref[target] = work_ref[target] + part
    before_ref[...] = work_ref[:owned]
    own_ref[...] = work_ref[owned : 2 * owned]
    after_ref[...] = work_ref[2 * owned :]


def aggregate(zone_by_slot, base, weight_blocks, cell_rows, owned_blocks):
    block_size = weight_blocks.shape[3]
    day_count = cell_rows.shape[2]
    table = jax.ShapeDtypeStruct((owned_blocks, block_size, day_count), jnp.float32)
    return pl.pallas_call(
        aggregate_kernel,
        out_shape=(table, table, table),
        in_specs=[
            pl.BlockSpec(memory_space=pltpu.SMEM),
            pl.BlockSpec(memory_space=pltpu.SMEM),
            pl.BlockSpec(memory_space=pltpu.VMEM),
            pl.BlockSpec(memory_space=pltpu.VMEM),
        ],
        out_specs=(
            pl.BlockSpec(memory_space=pltpu.VMEM),
            pl.BlockSpec(memory_space=pltpu.VMEM),
            pl.BlockSpec(memory_space=pltpu.VMEM),
        ),
        scratch_shapes=[pltpu.VMEM((3 * owned_blocks, block_size, day_count), jnp.float32)],
    )(zone_by_slot, base, weight_blocks, cell_rows)


def body(runoff, weight_blocks, block_zone, climatology, zone_weight):
    block_count = weight_blocks.shape[0]
    block_size = weight_blocks.shape[2]
    day_count = runoff.shape[1]
    owned_blocks = climatology.shape[0] // block_size
    device_count = lax.axis_size(DEVICE_AXES)
    device_index = lax.axis_index(DEVICE_AXES)
    cell_rows = runoff.reshape(block_count, block_size, day_count)
    base = jnp.reshape((device_index - 1) * owned_blocks, (1,)).astype(jnp.int32)
    to_before, own_table, to_after = aggregate(
        block_zone.astype(jnp.int32).T, base, weight_blocks, cell_rows, owned_blocks
    )
    from_before = shifted(to_after, DEVICE_AXES, 1)
    from_after = shifted(to_before, DEVICE_AXES, -1)
    summed = own_table + from_before + from_after
    aggregated = summed.reshape(owned_blocks * block_size, day_count)
    anomaly = zone_weight[:, None] * (aggregated - climatology)
    local_gram = jnp.dot(
        anomaly.T, anomaly, precision=exact_mode, preferred_element_type=jnp.float32
    )
    local_gram = 0.5 * (local_gram + local_gram.T)
    total_packed = all_sum(pack_gram(local_gram), device_count)
    root = math.sqrt(anomaly.shape[0] * device_count)
    factor, scores = cholesky_with_inverse(total_packed, anomaly, root)
    return (scores, factor)


def solution(mesh):
    return jax.shard_map(
        body,
        mesh=mesh,
        in_specs=(
            P(DEVICE_AXES, None),
            P(DEVICE_AXES, None, None, None),
            P(DEVICE_AXES, None),
            P(DEVICE_AXES, None),
            P(DEVICE_AXES),
        ),
        out_specs=(P(DEVICE_AXES, None), P()),
        check_vma=False,
    )
```
